32 devices in a mesh: dp: 8 (over y, x, core), space: 4 (over z).
Axes of the slice: x: 2, y: 2, z: 4, core: 2. Of those that a mesh axis runs over, the one named last changes fastest.
Arguments:
- volume: bfloat16 [8, 32, 8, 16, 128], P('dp', None, 'space')
- out_grad: bfloat16 [8, 32, 8, 16, 128], P('dp', None, 'space'), may hold values from -0.016479492 to 0.016479492
- kernel: bfloat16 [32, 864], replicated, may hold values from -0.21875 to 0.21875
- sample_idx: int32 [8, 4096], P('dp', 'space'), may hold values from 0 to 4095
- a_inverse: float32 [864, 864], P('space')
- g_inverse: float32 [32, 32], replicated
Outputs:
- conv_out: bfloat16 [8, 32, 8, 16, 128], P('dp', None, 'space')
- a_factor: float32 [864, 864], P('dp', 'space')
- g_factor: float32 [32, 32], replicated
- pre_grad: float32 [32, 864], replicated
The draws below stay inside these ranges and needn't reach their ends.
Inputs may be any that keep to these rules, and one draw needn't show every extreme that they name: `sample_idx`: column s of a sample's row names a cell of slab s // 1024, as the number z * 16 * 128 + y * 128 + x counted within that slab of 2 planes.
All inputs are finite; a program needn't handle non-finite values.
Results may differ from the reference program's by a relative error of at most 0.0085.
Values may be sent and summed in bfloat16 or wider, within the bound.
No kernel may reach another device: no remote copies, remote signals or barrier semaphores. Data moves between devices by JAX's collectives and lax.ppermute only.
A program may use at most 128 MiB of HBM per device.

```python
import jax
import jax.numpy as jnp
from jax import lax

C = 32
Z_DEV = 2
NY = 16
NX = 128
S_DEV = 1024
BATCH = 8
NZ = 8
PATCH = 864
SAMPLES = 4096
CELLS_DEV = 4096


def inverse_like(key, order):
    key_a = jax.random.fold_in(key, 11)
    key_b = jax.random.fold_in(key, 23)
    noise = jax.random.normal(key_a, (order, order), jnp.float32)
    diag = jax.random.uniform(key_b, (order,), jnp.float32, 0.5, 1.5)
    spread = 0.6
    symmetric = (noise + noise.T) * (0.5 * spread / order ** 0.5)
    return symmetric + jnp.diag(diag)


def draw_a_inverse(key, part):
    return inverse_like(key, PATCH)


def draw_g_inverse(key, part):
    return inverse_like(key, C)


def draw_volume(key, part):
    key_noise = jax.random.fold_in(key, 31)
    key_level = jax.random.fold_in(key, 37)
    key_sign = jax.random.fold_in(key, 41)
    key_owner = jax.random.fold_in(key, 43)
    shape = (BATCH, C, NZ, NY, NX)
    noise = jnp.clip(jax.random.normal(key_noise, shape, jnp.float32), -5.0, 5.0)
    level = jax.random.uniform(key_level, (C,), jnp.float32, 0.5, 1.0)
    signs = jnp.where(jax.random.bernoulli(key_sign, 0.5, (C,)), 1.0, -1.0).astype(jnp.float32)
    owner = jax.random.permutation(key_owner, BATCH).astype(jnp.int32)
    block_of = jnp.arange(C, dtype=jnp.int32) * BATCH // C
    boost = jnp.where(block_of[None, :] == owner[:, None], 3.0, 1.0).astype(jnp.float32)
    offset = (signs * level)[None, :, None, None, None]
    values = offset + noise * boost[:, :, None, None, None]
    return values.astype(jnp.bfloat16)


def touch_ends(values, own_key, smallest, top_value):
    longest = values.shape.index(max(values.shape))
    spots = []
    for shift in (0, 1):
        where = [jax.random.randint(jax.random.fold_in(own_key, axis), (), 0, length) for axis, length in enumerate(values.shape)]
        where[longest] = (where[longest] + shift) % values.shape[longest]
        spots.append(tuple(where))
    return values.at[spots[0]].set(smallest).at[spots[1]].set(top_value)


def with_spikes(drawn, key, source, target, blocks, factor):
    owner, partner = [(jnp.arange(drawn.shape[axis_at]) // (drawn.shape[axis_at] // blocks)).reshape([-1 if axis == axis_at else 1 for axis in range(drawn.ndim)]) for axis_at in (source, target)]
    chosen = jax.random.permutation(key, blocks)[partner]
    strong = (owner == chosen) | (owner == (partner + blocks // 2) % blocks)
    return jnp.where(strong, factor * drawn, drawn)


def block_levels(stream_key, extent, pieces, low, top_value):
    gain = 1.0
    for position, shards_of in pieces:
        steps = jax.random.uniform(jax.random.fold_in(jax.random.fold_in(stream_key, 6), position), (shards_of,), jnp.float32, low / len(pieces), top_value / len(pieces))
        gain = gain * jnp.repeat(jnp.exp(steps), extent[position] // shards_of).reshape((-1,) + (1,) * (len(extent) - 1 - position))
    return gain


def normal_values(key, dims, deviation, limit, shards=(), kind=jnp.bfloat16):
    loudness = block_levels(key, dims, shards, -0.22, 0.18) if shards else 1.0
    result = jax.random.normal(key, dims, jnp.float32) * deviation * loudness
    return jnp.minimum(jnp.maximum(result, -limit), limit).astype(kind)


def noise_with(own_key, shape, deviation, reach, split, heavy, held_as=jnp.bfloat16):
    result = deviation * jax.random.normal(own_key, shape, jnp.float32)
    if split:
        result = result * block_levels(own_key, shape, split, -0.22, 0.18)
    return jnp.clip(with_spikes(result, jax.random.fold_in(own_key, 3), *heavy), -reach, reach).astype(held_as)


def setup_inputs(seed: int = 0) -> dict:
    splits = jax.random.split(jax.random.key(seed), 7)
    return {
        "volume": draw_volume(jax.random.fold_in(splits[6], 71), 0),
        "out_grad": noise_with(splits[1], (BATCH, C, NZ, NY, NX), (1.0 / (BATCH * NZ * NY * NX) ** 0.5), 0.016479492, ((0, 8), (2, 4)), (0, 1, 8, 2.0)),
        "kernel": normal_values(splits[2], (C, PATCH), PATCH ** -0.5, 0.21875),
        "sample_idx": touch_ends(jax.random.randint(splits[3], (BATCH, SAMPLES), 0, CELLS_DEV), jax.random.fold_in(splits[3], 1), 0, CELLS_DEV - 1).astype(jnp.int32),
        "a_inverse": draw_a_inverse(jax.random.fold_in(splits[6], 71), 0),
        "g_inverse": draw_g_inverse(jax.random.fold_in(splits[6], 71), 0),
    }


def tap_list():
    return [(z_off, y_off, x_off) for z_off in range(3) for y_off in range(3) for x_off in range(3)]


def reference(volume, out_grad, kernel, sample_idx, a_inverse, g_inverse):
    highest = lax.Precision.HIGHEST
    kernel_taps = kernel.astype(jnp.float32).reshape(C, C, 27)
    offsets = jnp.arange(27)
    z_step = (offsets // 9).astype(jnp.int32)
    y_step = ((offsets // 3) % 3).astype(jnp.int32)
    x_step = (offsets % 3).astype(jnp.int32)
    slab_ids = (jnp.arange(SAMPLES) // S_DEV).astype(jnp.int32)

    def per_sample(carry, inputs):
        grad_sum, g_sum, a_sum = carry
        sample_vol, sample_grad, cell_ids = inputs
        padded = jnp.pad(sample_vol.astype(jnp.float32), ((0, 0), (1, 1), (1, 1), (1, 1)))
        grad_f = sample_grad.astype(jnp.float32)
        forward = jnp.zeros((C, NZ, NY, NX), jnp.float32)
        grad_taps = []
        for index, (z_off, y_off, x_off) in enumerate(tap_list()):
            shifted = padded[:, z_off:z_off + NZ, y_off:y_off + NY, x_off:x_off + NX]
            forward = forward + jnp.einsum("oc,czyx->ozyx", kernel_taps[:, :, index], shifted, precision=highest)
            grad_taps.append(jnp.einsum("ozyx,czyx->oc", grad_f, shifted, precision=highest))
        grad_w = jnp.stack(grad_taps, axis=2).reshape(C, PATCH)
        g_part = jnp.einsum("ozyx,pzyx->op", grad_f, grad_f, precision=highest)
        z_pos = (cell_ids // (NY * NX) + slab_ids * Z_DEV).astype(jnp.int32)
        y_pos = ((cell_ids // NX) % NY).astype(jnp.int32)
        x_pos = (cell_ids % NX).astype(jnp.int32)
        gathered = padded[:, z_pos[:, None] + z_step[None, :], y_pos[:, None] + y_step[None, :], x_pos[:, None] + x_step[None, :]]
        patches = jnp.transpose(gathered, (1, 0, 2)).reshape(SAMPLES, PATCH)
        a_part = jnp.dot(patches.T, patches, precision=highest)
        return (grad_sum + grad_w, g_sum + g_part, a_sum + a_part), forward.astype(jnp.bfloat16)

    start = (jnp.zeros((C, PATCH), jnp.float32), jnp.zeros((C, C), jnp.float32), jnp.zeros((PATCH, PATCH), jnp.float32))
    (grad_sum, g_factor, a_sum), conv_out = lax.scan(per_sample, start, (volume, out_grad, sample_idx))
    a_factor = a_sum / jnp.float32(BATCH * SAMPLES)
    left = jnp.dot(g_inverse, grad_sum, precision=highest)
    pre_grad = jnp.dot(left, a_inverse, precision=highest)
    return conv_out, a_factor, g_factor, pre_grad
```

```python
import jax
import jax.numpy as jnp
from jax import lax
from jax.sharding import PartitionSpec as P


def padded_2(cells, sides, width):
    for axis, dim in sides:
        count = lax.axis_size(axis)
        ends = count - 1
        head = lax.slice_in_dim(cells, 0, width, axis=dim)
        tail = lax.slice_in_dim(cells, cells.shape[dim] - width, cells.shape[dim], axis=dim)
        cells = jnp.concatenate(
            [
                lax.ppermute(tail, axis, [(i, (i + 1) % count) for i in range(ends)]),
                cells,
                lax.ppermute(head, axis, [((i + 1) % count, i) for i in range(ends)]),
            ],
            axis=dim,
        )
    return cells


def on_device(volume, out_grad, kernel, sample_idx, a_inverse, g_inverse):
    highest = lax.Precision.HIGHEST
    f32 = jnp.float32
    channels = volume.shape[1]
    planes = volume.shape[2]
    y_cells = volume.shape[3]
    x_cells = volume.shape[4]
    cells = planes * y_cells * x_cells
    patch = kernel.shape[1]
    n_dp = lax.axis_size("dp")
    n_sp = lax.axis_size("space")
    contract_cells = (((1,), (1,)), ((), ()))

    block = padded_2(volume, (("space", 2),), 1)
    padded = jnp.pad(block[0], ((0, 0), (0, 0), (1, 1), (1, 1)))
    taps = [
        padded[:, dz : dz + planes, dy : dy + y_cells, dx : dx + x_cells]
        for dz in range(3)
        for dy in range(3)
        for dx in range(3)
    ]
    patches_t = jnp.stack(taps, axis=1).reshape(patch, cells)
    grad_flat = out_grad[0].reshape(channels, cells)

    forward = jnp.dot(kernel, patches_t, preferred_element_type=f32)
    conv_out = forward.astype(jnp.bfloat16).reshape(1, channels, planes, y_cells, x_cells)
    grad_w = lax.dot_general(grad_flat, patches_t, contract_cells, preferred_element_type=f32)
    g_part = lax.dot_general(grad_flat, grad_flat, contract_cells, preferred_element_type=f32)

    cell_ids = sample_idx[0]
    counts = jnp.sum(
        (cell_ids[:, None] == jnp.arange(cells, dtype=jnp.int32)[None, :]).astype(f32), axis=0
    )
    weighted = patches_t.astype(f32) * counts[None, :]
    high = weighted.astype(jnp.bfloat16)
    low = (weighted - high.astype(f32)).astype(jnp.bfloat16)
    total_samples = sample_idx.shape[1] * n_sp * n_dp
    a_part = (
        lax.dot_general(high, patches_t, contract_cells, preferred_element_type=f32)
        + lax.dot_general(low, patches_t, contract_cells, preferred_element_type=f32)
    ) / jnp.float32(total_samples)
    rows = patch // n_dp
    cols = patch // n_sp
    a_blocks = (
        a_part.astype(jnp.bfloat16)
        .reshape(n_dp, rows, n_sp, cols)
        .transpose(0, 2, 1, 3)
        .reshape(n_dp * n_sp, rows, cols)
    )
    a_factor = lax.psum_scatter(a_blocks, ("dp", "space"), scatter_dimension=0, tiled=True)
    a_factor = a_factor.reshape(rows, cols).astype(f32)

    both = lax.psum(jnp.concatenate([grad_w, g_part], axis=1), ("dp", "space"))
    grad_sum = both[:, :patch]
    g_factor = both[:, patch:]
    left = jnp.dot(g_inverse, grad_sum, precision=highest)
    own_rows = a_inverse.shape[0]
    left_rows = lax.dynamic_slice_in_dim(left, lax.axis_index("space") * own_rows, own_rows, axis=1)
    pre_grad = lax.psum(jnp.dot(left_rows, a_inverse, precision=highest), "space")
    return (conv_out, a_factor, g_factor, pre_grad)


def solution(mesh):
    placed = (
        P("dp", None, "space", None, None),
        P("dp", None, "space", None, None),
        P(),
        P("dp", "space"),
        P("space", None),
        P(),
    )
    return jax.shard_map(
        on_device,
        mesh=mesh,
        in_specs=placed,
        out_specs=(P("dp", None, "space", None, None), P("dp", "space"), P(), P()),
        check_vma=False,
    )
```

```python
import jax
import jax.numpy as jnp
from jax import lax
from jax.sharding import PartitionSpec as P


def padded_2(cells, sides, width):
    for axis, dim in sides:
        count = lax.axis_size(axis)
        ends = count - 1
        head = lax.slice_in_dim(cells, 0, width, axis=dim)
        tail = lax.slice_in_dim(cells, cells.shape[dim] - width, cells.shape[dim], axis=dim)
        cells = jnp.concatenate(
            [
                lax.ppermute(tail, axis, [(i, (i + 1) % count) for i in range(ends)]),
                cells,
                lax.ppermute(head, axis, [((i + 1) % count, i) for i in range(ends)]),
            ],
            axis=dim,
        )
    return cells


def partner(axis, step):
    return [(i, i ^ step) for i in range(lax.axis_size(axis))]


def butterfly_sum(x, axes):
    for axis in axes:
        step = 1
        while step < lax.axis_size(axis):
            x = x + lax.ppermute(x, axis, partner(axis, step))
            step *= 2
    return x


def halving_scatter(blocks, axis, dim):
    me = lax.axis_index(axis)
    step = 1
    while step < lax.axis_size(axis):
        shape = blocks.shape
        split = blocks.reshape(shape[:dim] + (shape[dim] // 2, 2) + shape[dim + 1 :])
        bit = (me // step) % 2
        keep = lax.dynamic_index_in_dim(split, bit, axis=dim + 1, keepdims=False)
        send = lax.dynamic_index_in_dim(split, 1 - bit, axis=dim + 1, keepdims=False)
        got = lax.ppermute(send.astype(jnp.bfloat16), axis, partner(axis, step))
        blocks = keep + got.astype(jnp.float32)
        step *= 2
    return blocks


def doubling_gather(x, axis):
    me = lax.axis_index(axis)
    step = 1
    while step < lax.axis_size(axis):
        other = lax.ppermute(x, axis, partner(axis, step))
        first = (me // step) % 2 == 0
        x = jnp.where(first, jnp.concatenate([x, other]), jnp.concatenate([other, x]))
        step *= 2
    return x


def on_device(volume, out_grad, kernel, sample_idx, a_inverse, g_inverse):
    highest = lax.Precision.HIGHEST
    f32 = jnp.float32
    channels = volume.shape[1]
    planes = volume.shape[2]
    y_cells = volume.shape[3]
    x_cells = volume.shape[4]
    cells = planes * y_cells * x_cells
    patch = kernel.shape[1]
    n_taps = patch // channels
    n_dp = lax.axis_size("dp")
    n_sp = lax.axis_size("space")
    contract_cells = (((1,), (1,)), ((), ()))

    full_inverse = doubling_gather(a_inverse, "space")

    block = padded_2(volume, (("space", 2),), 1)
    padded = jnp.pad(block[0], ((0, 0), (0, 0), (1, 1), (1, 1)))
    taps = [
        padded[:, dz : dz + planes, dy : dy + y_cells, dx : dx + x_cells]
        for dz in range(3)
        for dy in range(3)
        for dx in range(3)
    ]
    patches_t = jnp.stack(taps, axis=0).reshape(patch, cells)
    grad_flat = out_grad[0].reshape(channels, cells)
    kernel_perm = kernel.reshape(channels, channels, n_taps).transpose(0, 2, 1).reshape(channels, patch)

    grad_perm = lax.dot_general(grad_flat, patches_t, contract_cells, preferred_element_type=f32)
    grad_w = grad_perm.reshape(channels, n_taps, channels).transpose(0, 2, 1).reshape(channels, patch)
    g_part = lax.dot_general(grad_flat, grad_flat, contract_cells, preferred_element_type=f32)
    both = butterfly_sum(jnp.concatenate([grad_w, g_part], axis=1), ("dp", "space"))
    grad_sum = both[:, :patch]
    g_factor = both[:, patch:]
    left = jnp.dot(g_inverse, grad_sum, precision=highest)
    pre_grad = jnp.dot(left, full_inverse, precision=highest)

    forward = jnp.dot(kernel_perm, patches_t, preferred_element_type=f32)
    conv_out = forward.astype(jnp.bfloat16).reshape(1, channels, planes, y_cells, x_cells)

    cell_ids = sample_idx[0]
    counts = jnp.sum(
        (cell_ids[:, None] == jnp.arange(cells, dtype=jnp.int32)[None, :]).astype(f32), axis=0
    )
    weighted = patches_t.astype(f32) * counts[None, :]
    high = weighted.astype(jnp.bfloat16)
    low = (weighted - high.astype(f32)).astype(jnp.bfloat16)
    total_samples = sample_idx.shape[1] * n_sp * n_dp
    a_perm = (
        lax.dot_general(high, patches_t, contract_cells, preferred_element_type=f32)
        + lax.dot_general(low, patches_t, contract_cells, preferred_element_type=f32)
    ) / jnp.float32(total_samples)
    a_part = (
        a_perm.reshape(n_taps, channels, n_taps, channels).transpose(1, 0, 3, 2).reshape(patch, patch)
    )
    rows = patch // n_dp
    cols = patch // n_sp
    a_rows = halving_scatter(a_part.reshape(n_dp, rows, patch), "dp", 0)
    a_factor = halving_scatter(a_rows.reshape(rows, n_sp, cols), "space", 1).reshape(rows, cols)
    return (conv_out, a_factor, g_factor, pre_grad)


def solution(mesh):
    placed = (
        P("dp", None, "space", None, None),
        P("dp", None, "space", None, None),
        P(),
        P("dp", "space"),
        P("space", None),
        P(),
    )
    return jax.shard_map(
        on_device,
        mesh=mesh,
        in_specs=placed,
        out_specs=(P("dp", None, "space", None, None), P("dp", "space"), P(), P()),
        check_vma=False,
    )
```

```python
import math

import jax
import jax.numpy as jnp
from jax import lax
from jax.sharding import PartitionSpec as P


def padded_2(cells, sides, width):
    for axis, dim in sides:
        count = lax.axis_size(axis)
        ends = count - 1
        head = lax.slice_in_dim(cells, 0, width, axis=dim)
        tail = lax.slice_in_dim(cells, cells.shape[dim] - width, cells.shape[dim], axis=dim)
        cells = jnp.concatenate(
            [
                lax.ppermute(tail, axis, [(i, (i + 1) % count) for i in range(ends)]),
                cells,
                lax.ppermute(head, axis, [((i + 1) % count, i) for i in range(ends)]),
            ],
            axis=dim,
        )
    return cells


def partner(axis, step):
    return [(i, i ^ step) for i in range(lax.axis_size(axis))]


def butterfly_sum(x, axes):
    for axis in axes:
        step = 1
        while step < lax.axis_size(axis):
            x = x + lax.ppermute(x, axis, partner(axis, step))
            step *= 2
    return x


def halving_scatter(blocks, axis, dim):
    me = lax.axis_index(axis)
    step = 1
    while step < lax.axis_size(axis):
        shape = blocks.shape
        split = blocks.reshape(shape[:dim] + (shape[dim] // 2, 2) + shape[dim + 1 :])
        bit = (me // step) % 2
        keep = lax.dynamic_index_in_dim(split, bit, axis=dim + 1, keepdims=False)
        send = lax.dynamic_index_in_dim(split, 1 - bit, axis=dim + 1, keepdims=False)
        got = lax.ppermute(send.astype(jnp.bfloat16), axis, partner(axis, step))
        blocks = keep + got.astype(jnp.float32)
        step *= 2
    return blocks


def doubling_gather(x, axis):
    me = lax.axis_index(axis)
    step = 1
    while step < lax.axis_size(axis):
        other = lax.ppermute(x, axis, partner(axis, step))
        first = (me // step) % 2 == 0
        x = jnp.where(first, jnp.concatenate([x, other]), jnp.concatenate([other, x]))
        step *= 2
    return x


def on_device(volume, out_grad, kernel, sample_idx, a_inverse, g_inverse):
    highest = lax.Precision.HIGHEST
    f32 = jnp.float32
    channels = volume.shape[1]
    planes = volume.shape[2]
    y_cells = volume.shape[3]
    x_cells = volume.shape[4]
    cells = planes * y_cells * x_cells
    patch = kernel.shape[1]
    n_taps = patch // channels
    n_dp = lax.axis_size("dp")
    n_sp = lax.axis_size("space")
    row_ch = channels // n_dp
    col_ch = channels // n_sp
    grain = math.gcd(row_ch, col_ch)
    n_grains = channels // grain
    contract_cells = (((1,), (1,)), ((), ()))

    full_inverse = lax.all_gather(a_inverse, "space", axis=0, tiled=True)

    block = padded_2(volume, (("space", 2),), 1)
    padded = jnp.pad(block[0], ((0, 0), (0, 0), (1, 1), (1, 1)))
    grains = padded.reshape((n_grains, grain) + padded.shape[1:])
    taps = [
        grains[:, :, dz : dz + planes, dy : dy + y_cells, dx : dx + x_cells]
        for dz in range(3)
        for dy in range(3)
        for dx in range(3)
    ]
    patches_t = jnp.stack(taps, axis=1).reshape(patch, cells)
    patches_t = lax.optimization_barrier(patches_t)
    grad_flat = out_grad[0].reshape(channels, cells)
    kernel_perm = (
        kernel.reshape(channels, n_grains, grain, n_taps).transpose(0, 1, 3, 2).reshape(channels, patch)
    )

    grad_perm = lax.dot_general(grad_flat, patches_t, contract_cells, preferred_element_type=f32)
    grad_w = (
        grad_perm.reshape(channels, n_grains, n_taps, grain).transpose(0, 1, 3, 2).reshape(channels, patch)
    )
    g_part = lax.dot_general(grad_flat, grad_flat, contract_cells, preferred_element_type=f32)
    both = butterfly_sum(jnp.concatenate([grad_w, g_part], axis=1), ("dp", "space"))
    grad_sum = both[:, :patch]
    g_factor = both[:, patch:]
    left = jnp.dot(g_inverse, grad_sum, precision=highest)
    pre_grad = jnp.dot(left, full_inverse, precision=highest)

    forward = jnp.dot(kernel_perm, patches_t, preferred_element_type=f32)
    conv_out = forward.astype(jnp.bfloat16).reshape(1, channels, planes, y_cells, x_cells)

    cell_ids = sample_idx[0]
    counts = jnp.sum(
        (cell_ids[:, None] == jnp.arange(cells, dtype=jnp.int32)[None, :]).astype(f32), axis=0
    )
    weighted = patches_t.astype(f32) * counts[None, :]
    high = weighted.astype(jnp.bfloat16)
    low = (weighted - high.astype(f32)).astype(jnp.bfloat16)
    total_samples = sample_idx.shape[1] * n_sp * n_dp
    a_perm = (
        lax.dot_general(high, patches_t, contract_cells, preferred_element_type=f32)
        + lax.dot_general(low, patches_t, contract_cells, preferred_element_type=f32)
    ) / jnp.float32(total_samples)
    rows = patch // n_dp
    cols = patch // n_sp
    a_blocks = (
        a_perm.astype(jnp.bfloat16)
        .reshape(n_dp, rows, n_sp, cols)
        .transpose(0, 2, 1, 3)
        .reshape(n_dp * n_sp, rows, cols)
    )
    got = lax.all_to_all(a_blocks, ("dp", "space"), 0, 0, tiled=True)
    a_own = jnp.sum(got.astype(f32), axis=0)
    a_factor = (
        a_own.reshape(row_ch // grain, n_taps, grain, col_ch // grain, n_taps, grain)
        .transpose(0, 2, 1, 3, 5, 4)
        .reshape(rows, cols)
    )
    return (conv_out, a_factor, g_factor, pre_grad)


def solution(mesh):
    placed = (
        P("dp", None, "space", None, None),
        P("dp", None, "space", None, None),
        P(),
        P("dp", "space"),
        P("space", None),
        P(),
    )
    return jax.shard_map(
        on_device,
        mesh=mesh,
        in_specs=placed,
        out_specs=(P("dp", None, "space", None, None), P("dp", "space"), P(), P()),
        check_vma=False,
    )
```

```python
import math

import jax
import jax.numpy as jnp
from jax import lax
from jax.sharding import PartitionSpec as P


def padded_2(cells, sides, width):
    for axis, dim in sides:
        count = lax.axis_size(axis)
        ends = count - 1
        head = lax.slice_in_dim(cells, 0, width, axis=dim)
        tail = lax.slice_in_dim(cells, cells.shape[dim] - width, cells.shape[dim], axis=dim)
        cells = jnp.concatenate(
            [
                lax.ppermute(tail, axis, [(i, (i + 1) % count) for i in range(ends)]),
                cells,
                lax.ppermute(head, axis, [((i + 1) % count, i) for i in range(ends)]),
            ],
            axis=dim,
        )
    return cells


def partner(axis, step):
    return [(i, i ^ step) for i in range(lax.axis_size(axis))]


def butterfly_sum(x, axes):
    for axis in axes:
        step = 1
        while step < lax.axis_size(axis):
            x = x + lax.ppermute(x, axis, partner(axis, step))
            step *= 2
    return x


def halving_scatter(blocks, axis, dim):
    me = lax.axis_index(axis)
    step = 1
    while step < lax.axis_size(axis):
        shape = blocks.shape
        split = blocks.reshape(shape[:dim] + (shape[dim] // 2, 2) + shape[dim + 1 :])
        bit = (me // step) % 2
        keep = lax.dynamic_index_in_dim(split, bit, axis=dim + 1, keepdims=False)
        send = lax.dynamic_index_in_dim(split, 1 - bit, axis=dim + 1, keepdims=False)
        got = lax.ppermute(send.astype(jnp.bfloat16), axis, partner(axis, step))
        blocks = keep + got.astype(jnp.float32)
        step *= 2
    return blocks


def doubling_gather(x, axis):
    me = lax.axis_index(axis)
    step = 1
    while step < lax.axis_size(axis):
        other = lax.ppermute(x, axis, partner(axis, step))
        first = (me // step) % 2 == 0
        x = jnp.where(first, jnp.concatenate([x, other]), jnp.concatenate([other, x]))
        step *= 2
    return x


def block_order(n_grains, n_taps, grain):
    size = n_grains * n_taps * grain
    old = jnp.arange(size, dtype=jnp.int32)
    new = ((old // (n_taps * grain)) * grain + old % grain) * n_taps + (old // grain) % n_taps
    return (jnp.arange(size, dtype=jnp.int32)[:, None] == new[None, :]).astype(jnp.float32)


def on_device(volume, out_grad, kernel, sample_idx, a_inverse, g_inverse):
    highest = lax.Precision.HIGHEST
    f32 = jnp.float32
    channels = volume.shape[1]
    planes = volume.shape[2]
    y_cells = volume.shape[3]
    x_cells = volume.shape[4]
    cells = planes * y_cells * x_cells
    patch = kernel.shape[1]
    n_taps = patch // channels
    n_dp = lax.axis_size("dp")
    n_sp = lax.axis_size("space")
    row_ch = channels // n_dp
    col_ch = channels // n_sp
    grain = math.gcd(row_ch, col_ch)
    n_grains = channels // grain
    contract_cells = (((1,), (1,)), ((), ()))

    own = a_inverse.shape[0] // grain // n_taps
    own_rows = a_inverse.reshape(own, grain, n_taps, patch).transpose(0, 2, 1, 3).reshape(-1, patch)
    inverse_rows = lax.all_gather(own_rows, "space", axis=0, tiled=True)

    block = padded_2(volume, (("space", 2),), 1)
    padded = jnp.pad(block[0], ((0, 0), (0, 0), (1, 1), (1, 1)))
    grains = padded.reshape((n_grains, grain) + padded.shape[1:])
    taps = [
        grains[:, :, dz : dz + planes, dy : dy + y_cells, dx : dx + x_cells]
        for dz in range(3)
        for dy in range(3)
        for dx in range(3)
    ]
    patches_t = jnp.stack(taps, axis=1).reshape(patch, cells)
    grad_flat = out_grad[0].reshape(channels, cells)
    kernel_perm = (
        kernel.reshape(channels, n_grains, grain, n_taps).transpose(0, 1, 3, 2).reshape(channels, patch)
    )

    grad_perm = lax.dot_general(grad_flat, patches_t, contract_cells, preferred_element_type=f32)
    g_part = lax.dot_general(grad_flat, grad_flat, contract_cells, preferred_element_type=f32)
    terms = jnp.concatenate([grad_perm, g_part], axis=1)
    terms, patches_t = lax.optimization_barrier((terms, patches_t))
    both = butterfly_sum(terms, ("dp", "space"))
    grad_sum = both[:, :patch]
    g_factor = both[:, patch:]
    left = jnp.dot(g_inverse, grad_sum, precision=highest)
    pre_grad = jnp.dot(left, inverse_rows, precision=highest)

    forward = jnp.dot(kernel_perm, patches_t, preferred_element_type=f32)
    conv_out = forward.astype(jnp.bfloat16).reshape(1, channels, planes, y_cells, x_cells)

    cell_ids = sample_idx[0]
    counts = jnp.sum(
        (cell_ids[:, None] == jnp.arange(cells, dtype=jnp.int32)[None, :]).astype(f32), axis=0
    )
    weighted = patches_t.astype(f32) * counts[None, :]
    high = weighted.astype(jnp.bfloat16)
    low = (weighted - high.astype(f32)).astype(jnp.bfloat16)
    total_samples = sample_idx.shape[1] * n_sp * n_dp
    a_perm = (
        lax.dot_general(high, patches_t, contract_cells, preferred_element_type=f32)
        + lax.dot_general(low, patches_t, contract_cells, preferred_element_type=f32)
    ) / jnp.float32(total_samples)
    rows = patch // n_dp
    cols = patch // n_sp
    a_blocks = (
        a_perm.astype(jnp.bfloat16)
        .reshape(n_dp, rows, n_sp, cols)
        .transpose(0, 2, 1, 3)
        .reshape(n_dp * n_sp, rows, cols)
    )
    got = lax.all_to_all(a_blocks, ("dp", "space"), 0, 0, tiled=True)
    a_own = jnp.sum(got.astype(f32), axis=0)
    a_factor = jnp.dot(
        jnp.dot(block_order(row_ch // grain, n_taps, grain), a_own, precision=highest),
        block_order(col_ch // grain, n_taps, grain).T,
        precision=highest,
    )
    return (conv_out, a_factor, g_factor, pre_grad)


def solution(mesh):
    placed = (
        P("dp", None, "space", None, None),
        P("dp", None, "space", None, None),
        P(),
        P("dp", "space"),
        P("space", None),
        P(),
    )
    return jax.shard_map(
        on_device,
        mesh=mesh,
        in_specs=placed,
        out_specs=(P("dp", None, "space", None, None), P("dp", "space"), P(), P()),
        check_vma=False,
    )
```

```python
import math

import jax
import jax.numpy as jnp
from jax import lax
from jax.sharding import PartitionSpec as P


def padded_2(cells, sides, width):
    for axis, dim in sides:
        count = lax.axis_size(axis)
        ends = count - 1
        head = lax.slice_in_dim(cells, 0, width, axis=dim)
        tail = lax.slice_in_dim(cells, cells.shape[dim] - width, cells.shape[dim], axis=dim)
        cells = jnp.concatenate(
            [
                lax.ppermute(tail, axis, [(i, (i + 1) % count) for i in range(ends)]),
                cells,
                lax.ppermute(head, axis, [((i + 1) % count, i) for i in range(ends)]),
            ],
            axis=dim,
        )
    return cells


def partner(axis, step):
    return [(i, i ^ step) for i in range(lax.axis_size(axis))]


def butterfly_sum(x, axes):
    for axis in axes:
        step = 1
        while step < lax.axis_size(axis):
            x = x + lax.ppermute(x, axis, partner(axis, step))
            step *= 2
    return x


def halving_scatter(blocks, axis, dim):
    me = lax.axis_index(axis)
    step = 1
    while step < lax.axis_size(axis):
        shape = blocks.shape
        split = blocks.reshape(shape[:dim] + (shape[dim] // 2, 2) + shape[dim + 1 :])
        bit = (me // step) % 2
        keep = lax.dynamic_index_in_dim(split, bit, axis=dim + 1, keepdims=False)
        send = lax.dynamic_index_in_dim(split, 1 - bit, axis=dim + 1, keepdims=False)
        got = lax.ppermute(send.astype(jnp.bfloat16), axis, partner(axis, step))
        blocks = keep + got.astype(jnp.float32)
        step *= 2
    return blocks


def doubling_gather(x, axis):
    me = lax.axis_index(axis)
    step = 1
    while step < lax.axis_size(axis):
        other = lax.ppermute(x, axis, partner(axis, step))
        first = (me // step) % 2 == 0
        x = jnp.where(first, jnp.concatenate([x, other]), jnp.concatenate([other, x]))
        step *= 2
    return x


def exchange_sum(x, axes, n):
    width = x.shape[1]
    piece = -(-width // n)
    x = jnp.pad(x, ((0, 0), (0, piece * n - width)))
    parts = x.reshape(x.shape[0], n, piece).transpose(1, 0, 2)
    mine = jnp.sum(lax.all_to_all(parts, axes, 0, 0, tiled=True), axis=0)
    back = lax.all_to_all(jnp.broadcast_to(mine[None], (n,) + mine.shape), axes, 0, 0, tiled=True)
    return back.transpose(1, 0, 2).reshape(x.shape[0], n * piece)[:, :width]


def block_order(n_grains, n_taps, grain):
    size = n_grains * n_taps * grain
    old = jnp.arange(size, dtype=jnp.int32)
    new = ((old // (n_taps * grain)) * grain + old % grain) * n_taps + (old // grain) % n_taps
    return (jnp.arange(size, dtype=jnp.int32)[:, None] == new[None, :]).astype(jnp.float32)


def on_device(volume, out_grad, kernel, sample_idx, a_inverse, g_inverse):
    highest = lax.Precision.HIGHEST
    f32 = jnp.float32
    channels = volume.shape[1]
    planes = volume.shape[2]
    y_cells = volume.shape[3]
    x_cells = volume.shape[4]
    cells = planes * y_cells * x_cells
    patch = kernel.shape[1]
    n_taps = patch // channels
    n_dp = lax.axis_size("dp")
    n_sp = lax.axis_size("space")
    row_ch = channels // n_dp
    col_ch = channels // n_sp
    grain = math.gcd(row_ch, col_ch)
    n_grains = channels // grain
    contract_cells = (((1,), (1,)), ((), ()))

    own = a_inverse.shape[0] // grain // n_taps
    own_rows = a_inverse.reshape(own, grain, n_taps, patch).transpose(0, 2, 1, 3).reshape(-1, patch)
    inverse_rows = lax.all_to_all(
        jnp.broadcast_to(own_rows[None], (n_sp,) + own_rows.shape), "space", 0, 0, tiled=True
    ).reshape(patch, patch)

    block = padded_2(volume, (("space", 2),), 1)
    padded = jnp.pad(block[0], ((0, 0), (0, 0), (1, 1), (1, 1)))
    grains = padded.reshape((n_grains, grain) + padded.shape[1:])
    taps = [
        grains[:, :, dz : dz + planes, dy : dy + y_cells, dx : dx + x_cells]
        for dz in range(3)
        for dy in range(3)
        for dx in range(3)
    ]
    patches_t = jnp.stack(taps, axis=1).reshape(patch, cells)
    grad_flat = out_grad[0].reshape(channels, cells)
    kernel_perm = (
        kernel.reshape(channels, n_grains, grain, n_taps).transpose(0, 1, 3, 2).reshape(channels, patch)
    )

    grad_perm = lax.dot_general(grad_flat, patches_t, contract_cells, preferred_element_type=f32)
    g_part = lax.dot_general(grad_flat, grad_flat, contract_cells, preferred_element_type=f32)
    terms = jnp.concatenate([grad_perm, g_part], axis=1)
    terms, patches_t = lax.optimization_barrier((terms, patches_t))
    both = exchange_sum(terms, ("dp", "space"), n_dp * n_sp)
    grad_sum = both[:, :patch]
    g_factor = both[:, patch:]
    left = jnp.dot(g_inverse, grad_sum, precision=highest)
    pre_grad = jnp.dot(left, inverse_rows, precision=highest)

    forward = jnp.dot(kernel_perm, patches_t, preferred_element_type=f32)
    conv_out = forward.astype(jnp.bfloat16).reshape(1, channels, planes, y_cells, x_cells)

    cell_ids = sample_idx[0]
    counts = jnp.sum(
        (cell_ids[:, None] == jnp.arange(cells, dtype=jnp.int32)[None, :]).astype(f32), axis=0
    )
    weighted = patches_t.astype(f32) * counts[None, :]
    high = weighted.astype(jnp.bfloat16)
    low = (weighted - high.astype(f32)).astype(jnp.bfloat16)
    total_samples = sample_idx.shape[1] * n_sp * n_dp
    a_perm = (
        lax.dot_general(high, patches_t, contract_cells, preferred_element_type=f32)
        + lax.dot_general(low, patches_t, contract_cells, preferred_element_type=f32)
    ) / jnp.float32(total_samples)
    rows = patch // n_dp
    cols = patch // n_sp
    a_blocks = (
        a_perm.astype(jnp.bfloat16)
        .reshape(n_dp, rows, n_sp, cols)
        .transpose(0, 2, 1, 3)
        .reshape(n_dp * n_sp, rows, cols)
    )
    got = lax.all_to_all(a_blocks, ("dp", "space"), 0, 0, tiled=True)
    a_own = jnp.sum(got.astype(f32), axis=0)
    a_factor = jnp.dot(
        jnp.dot(block_order(row_ch // grain, n_taps, grain), a_own, precision=highest),
        block_order(col_ch // grain, n_taps, grain).T,
        precision=highest,
    )
    return (conv_out, a_factor, g_factor, pre_grad)


def solution(mesh):
    placed = (
        P("dp", None, "space", None, None),
        P("dp", None, "space", None, None),
        P(),
        P("dp", "space"),
        P("space", None),
        P(),
    )
    return jax.shard_map(
        on_device,
        mesh=mesh,
        in_specs=placed,
        out_specs=(P("dp", None, "space", None, None), P("dp", "space"), P(), P()),
        check_vma=False,
    )
```

```python
import math

import jax
import jax.numpy as jnp
from jax import lax
from jax.sharding import PartitionSpec as P


def padded_2(cells, sides, width):
    for axis, dim in sides:
        count = lax.axis_size(axis)
        ends = count - 1
        head = lax.slice_in_dim(cells, 0, width, axis=dim)
        tail = lax.slice_in_dim(cells, cells.shape[dim] - width, cells.shape[dim], axis=dim)
        cells = jnp.concatenate(
            [
                lax.ppermute(tail, axis, [(i, (i + 1) % count) for i in range(ends)]),
                cells,
                lax.ppermute(head, axis, [((i + 1) % count, i) for i in range(ends)]),
            ],
            axis=dim,
        )
    return cells


def partner(axis, step):
    return [(i, i ^ step) for i in range(lax.axis_size(axis))]


def butterfly_sum(x, axes):
    for axis in axes:
        step = 1
        while step < lax.axis_size(axis):
            x = x + lax.ppermute(x, axis, partner(axis, step))
            step *= 2
    return x


def halving_scatter(blocks, axis, dim):
    me = lax.axis_index(axis)
    step = 1
    while step < lax.axis_size(axis):
        shape = blocks.shape
        split = blocks.reshape(shape[:dim] + (shape[dim] // 2, 2) + shape[dim + 1 :])
        bit = (me // step) % 2
        keep = lax.dynamic_index_in_dim(split, bit, axis=dim + 1, keepdims=False)
        send = lax.dynamic_index_in_dim(split, 1 - bit, axis=dim + 1, keepdims=False)
        got = lax.ppermute(send.astype(jnp.bfloat16), axis, partner(axis, step))
        blocks = keep + got.astype(jnp.float32)
        step *= 2
    return blocks


def doubling_gather(x, axis):
    me = lax.axis_index(axis)
    step = 1
    while step < lax.axis_size(axis):
        other = lax.ppermute(x, axis, partner(axis, step))
        first = (me // step) % 2 == 0
        x = jnp.where(first, jnp.concatenate([x, other]), jnp.concatenate([other, x]))
        step *= 2
    return x


def tap_order(channels, n_taps):
    size = channels * n_taps
    new = jnp.arange(size, dtype=jnp.int32)
    old = (new % n_taps) * channels + new // n_taps
    return (old[:, None] == jnp.arange(size, dtype=jnp.int32)[None, :]).astype(jnp.bfloat16)


def block_order(n_grains, n_taps, grain):
    size = n_grains * n_taps * grain
    old = jnp.arange(size, dtype=jnp.int32)
    new = ((old // (n_taps * grain)) * grain + old % grain) * n_taps + (old // grain) % n_taps
    return (jnp.arange(size, dtype=jnp.int32)[:, None] == new[None, :]).astype(jnp.float32)


def on_device(volume, out_grad, kernel, sample_idx, a_inverse, g_inverse):
    highest = lax.Precision.HIGHEST
    f32 = jnp.float32
    channels = volume.shape[1]
    planes = volume.shape[2]
    y_cells = volume.shape[3]
    x_cells = volume.shape[4]
    cells = planes * y_cells * x_cells
    patch = kernel.shape[1]
    n_taps = patch // channels
    n_dp = lax.axis_size("dp")
    n_sp = lax.axis_size("space")
    row_ch = channels // n_dp
    col_ch = channels // n_sp
    grain = math.gcd(row_ch, col_ch)
    n_grains = channels // grain
    contract_cells = (((1,), (1,)), ((), ()))

    full_inverse = lax.all_gather(a_inverse, "space", axis=0, tiled=True)

    block = padded_2(volume, (("space", 2),), 1)
    padded = jnp.pad(block[0], ((0, 0), (0, 0), (1, 1), (1, 1)))
    slab = jnp.transpose(padded, (1, 2, 0, 3))
    taps = [
        slab[dz : dz + planes, dy : dy + y_cells, :, dx : dx + x_cells]
        for dz in range(3)
        for dy in range(3)
        for dx in range(3)
    ]
    patches_t = jnp.stack(taps, axis=0).transpose(0, 3, 1, 2, 4).reshape(patch, cells)
    grad_flat = out_grad[0].reshape(channels, cells)
    kernel_perm = kernel.reshape(channels, channels, n_taps).transpose(0, 2, 1).reshape(channels, patch)

    grad_perm = lax.dot_general(grad_flat, patches_t, contract_cells, preferred_element_type=f32)
    g_part = lax.dot_general(grad_flat, grad_flat, contract_cells, preferred_element_type=f32)
    terms = jnp.concatenate([grad_perm, g_part], axis=1)
    terms, patches_t = lax.optimization_barrier((terms, patches_t))
    both = butterfly_sum(terms, ("dp", "space"))
    grad_sum = (
        both[:, :patch].reshape(channels, n_taps, channels).transpose(0, 2, 1).reshape(channels, patch)
    )
    g_factor = both[:, patch:]
    left = jnp.dot(g_inverse, grad_sum, precision=highest)
    pre_grad = jnp.dot(left, full_inverse, precision=highest)

    forward = jnp.dot(kernel_perm, patches_t, preferred_element_type=f32)
    conv_out = forward.astype(jnp.bfloat16).reshape(1, channels, planes, y_cells, x_cells)

    cell_ids = sample_idx[0]
    counts = jnp.sum(
        (cell_ids[:, None] == jnp.arange(cells, dtype=jnp.int32)[None, :]).astype(f32), axis=0
    )
    weighted = patches_t.astype(f32) * counts[None, :]
    high = weighted.astype(jnp.bfloat16)
    low = (weighted - high.astype(f32)).astype(jnp.bfloat16)
    total_samples = sample_idx.shape[1] * n_sp * n_dp
    a_perm = (
        lax.dot_general(high, patches_t, contract_cells, preferred_element_type=f32)
        + lax.dot_general(low, patches_t, contract_cells, preferred_element_type=f32)
    ) / jnp.float32(total_samples)
    order = tap_order(channels, n_taps)
    a_rows = jnp.dot(order, a_perm.astype(jnp.bfloat16), preferred_element_type=f32)
    a_orig = lax.dot_general(
        a_rows.astype(jnp.bfloat16), order, contract_cells, preferred_element_type=f32
    ).astype(jnp.bfloat16)
    rows = patch // n_dp
    cols = patch // n_sp
    a_blocks = (
        a_orig.reshape(n_dp, rows, n_sp, cols).transpose(0, 2, 1, 3).reshape(n_dp * n_sp, rows, cols)
    )
    a_blocks, pre_grad, g_factor = lax.optimization_barrier((a_blocks, pre_grad, g_factor))
    got = lax.all_to_all(a_blocks, ("dp", "space"), 0, 0, tiled=True)
    a_factor = jnp.sum(got.astype(f32), axis=0)
    return (conv_out, a_factor, g_factor, pre_grad)


def solution(mesh):
    placed = (
        P("dp", None, "space", None, None),
        P("dp", None, "space", None, None),
        P(),
        P("dp", "space"),
        P("space", None),
        P(),
    )
    return jax.shard_map(
        on_device,
        mesh=mesh,
        in_specs=placed,
        out_specs=(P("dp", None, "space", None, None), P("dp", "space"), P(), P()),
        check_vma=False,
    )
```

```python
import math

import jax
import jax.numpy as jnp
from jax import lax
from jax.sharding import PartitionSpec as P


def padded_2(cells, sides, width):
    for axis, dim in sides:
        count = lax.axis_size(axis)
        ends = count - 1
        head = lax.slice_in_dim(cells, 0, width, axis=dim)
        tail = lax.slice_in_dim(cells, cells.shape[dim] - width, cells.shape[dim], axis=dim)
        cells = jnp.concatenate(
            [
                lax.ppermute(tail, axis, [(i, (i + 1) % count) for i in range(ends)]),
                cells,
                lax.ppermute(head, axis, [((i + 1) % count, i) for i in range(ends)]),
            ],
            axis=dim,
        )
    return cells


def partner(axis, step):
    return [(i, i ^ step) for i in range(lax.axis_size(axis))]


def butterfly_sum(x, axes):
    for axis in axes:
        step = 1
        while step < lax.axis_size(axis):
            x = x + lax.ppermute(x, axis, partner(axis, step))
            step *= 2
    return x


def halving_scatter(blocks, axis, dim):
    me = lax.axis_index(axis)
    step = 1
    while step < lax.axis_size(axis):
        shape = blocks.shape
        split = blocks.reshape(shape[:dim] + (shape[dim] // 2, 2) + shape[dim + 1 :])
        bit = (me // step) % 2
        keep = lax.dynamic_index_in_dim(split, bit, axis=dim + 1, keepdims=False)
        send = lax.dynamic_index_in_dim(split, 1 - bit, axis=dim + 1, keepdims=False)
        got = lax.ppermute(send.astype(jnp.bfloat16), axis, partner(axis, step))
        blocks = keep + got.astype(jnp.float32)
        step *= 2
    return blocks


def doubling_gather(x, axis):
    me = lax.axis_index(axis)
    step = 1
    while step < lax.axis_size(axis):
        other = lax.ppermute(x, axis, partner(axis, step))
        first = (me // step) % 2 == 0
        x = jnp.where(first, jnp.concatenate([x, other]), jnp.concatenate([other, x]))
        step *= 2
    return x


def tap_order(channels, n_taps):
    size = channels * n_taps
    new = jnp.arange(size, dtype=jnp.int32)
    old = (new % n_taps) * channels + new // n_taps
    return (old[:, None] == jnp.arange(size, dtype=jnp.int32)[None, :]).astype(jnp.bfloat16)


def block_order(n_grains, n_taps, grain):
    size = n_grains * n_taps * grain
    old = jnp.arange(size, dtype=jnp.int32)
    new = ((old // (n_taps * grain)) * grain + old % grain) * n_taps + (old // grain) % n_taps
    return (jnp.arange(size, dtype=jnp.int32)[:, None] == new[None, :]).astype(jnp.float32)


def on_device(volume, out_grad, kernel, sample_idx, a_inverse, g_inverse):
    highest = lax.Precision.HIGHEST
    f32 = jnp.float32
    channels = volume.shape[1]
    planes = volume.shape[2]
    y_cells = volume.shape[3]
    x_cells = volume.shape[4]
    cells = planes * y_cells * x_cells
    patch = kernel.shape[1]
    n_taps = patch // channels
    n_dp = lax.axis_size("dp")
    n_sp = lax.axis_size("space")
    row_ch = channels // n_dp
    col_ch = channels // n_sp
    grain = math.gcd(row_ch, col_ch)
    n_grains = channels // grain
    contract_cells = (((1,), (1,)), ((), ()))

    full_inverse = lax.all_gather(a_inverse, "space", axis=0, tiled=True)

    block = padded_2(volume, (("space", 2),), 1)
    padded = jnp.pad(block[0], ((0, 0), (0, 0), (1, 1), (1, 1)))
    slab = jnp.transpose(padded, (1, 2, 0, 3))
    taps = [
        slab[dz : dz + planes, dy : dy + y_cells, :, dx : dx + x_cells]
        for dz in range(3)
        for dy in range(3)
        for dx in range(3)
    ]
    patches_t = jnp.stack(taps, axis=0).transpose(0, 3, 1, 2, 4).reshape(patch, cells)
    grad_flat = out_grad[0].reshape(channels, cells)
    kernel_perm = kernel.reshape(channels, channels, n_taps).transpose(0, 2, 1).reshape(channels, patch)

    grad_perm = lax.dot_general(grad_flat, patches_t, contract_cells, preferred_element_type=f32)
    g_part = lax.dot_general(grad_flat, grad_flat, contract_cells, preferred_element_type=f32)
    terms = jnp.concatenate([grad_perm, g_part], axis=1)
    terms, patches_t = lax.optimization_barrier((terms, patches_t))
    both = butterfly_sum(terms, ("dp", "space"))
    grad_sum = (
        both[:, :patch].reshape(channels, n_taps, channels).transpose(0, 2, 1).reshape(channels, patch)
    )
    g_factor = both[:, patch:]
    left = jnp.dot(g_inverse, grad_sum, precision=highest)
    pre_grad = jnp.dot(left, full_inverse, precision=highest)

    forward = jnp.dot(kernel_perm, patches_t, preferred_element_type=f32)
    conv_out = forward.astype(jnp.bfloat16).reshape(1, channels, planes, y_cells, x_cells)

    cell_ids = sample_idx[0]
    counts = jnp.sum(
        (cell_ids[:, None] == jnp.arange(cells, dtype=jnp.int32)[None, :]).astype(f32), axis=0
    )
    weighted = patches_t.astype(f32) * counts[None, :]
    high = weighted.astype(jnp.bfloat16)
    low = (weighted - high.astype(f32)).astype(jnp.bfloat16)
    total_samples = sample_idx.shape[1] * n_sp * n_dp
    a_perm = (
        lax.dot_general(high, patches_t, contract_cells, preferred_element_type=f32)
        + lax.dot_general(low, patches_t, contract_cells, preferred_element_type=f32)
    ) / jnp.float32(total_samples)
    order = tap_order(channels, n_taps)
    a_rows = jnp.dot(order, a_perm.astype(jnp.bfloat16), preferred_element_type=f32)
    a_orig = lax.dot_general(
        a_rows.astype(jnp.bfloat16), order, contract_cells, preferred_element_type=f32
    ).astype(jnp.bfloat16)
    rows = patch // n_dp
    cols = patch // n_sp
    a_blocks = (
        a_orig.reshape(n_dp, rows, n_sp, cols).transpose(0, 2, 1, 3).reshape(n_dp * n_sp, rows, cols)
    )
    got = lax.all_to_all(a_blocks, ("dp", "space"), 0, 0, tiled=True)
    a_factor = jnp.sum(got.astype(f32), axis=0)
    return (conv_out, a_factor, g_factor, pre_grad)


def solution(mesh):
    placed = (
        P("dp", None, "space", None, None),
        P("dp", None, "space", None, None),
        P(),
        P("dp", "space"),
        P("space", None),
        P(),
    )
    return jax.shard_map(
        on_device,
        mesh=mesh,
        in_specs=placed,
        out_specs=(P("dp", None, "space", None, None), P("dp", "space"), P(), P()),
        check_vma=False,
    )
```

```python
import math

import jax
import jax.numpy as jnp
from jax import lax
from jax.experimental import pallas as pl
from jax.sharding import PartitionSpec as P


def padded_2(cells, sides, width):
    for axis, dim in sides:
        count = lax.axis_size(axis)
        ends = count - 1
        head = lax.slice_in_dim(cells, 0, width, axis=dim)
        tail = lax.slice_in_dim(cells, cells.shape[dim] - width, cells.shape[dim], axis=dim)
        cells = jnp.concatenate(
            [
                lax.ppermute(tail, axis, [(i, (i + 1) % count) for i in range(ends)]),
                cells,
                lax.ppermute(head, axis, [((i + 1) % count, i) for i in range(ends)]),
            ],
            axis=dim,
        )
    return cells


def partner(axis, step):
    return [(i, i ^ step) for i in range(lax.axis_size(axis))]


def butterfly_sum(x, axes):
    for axis in axes:
        step = 1
        while step < lax.axis_size(axis):
            x = x + lax.ppermute(x, axis, partner(axis, step))
            step *= 2
    return x


def halving_scatter(blocks, axis, dim):
    me = lax.axis_index(axis)
    step = 1
    while step < lax.axis_size(axis):
        shape = blocks.shape
        split = blocks.reshape(shape[:dim] + (shape[dim] // 2, 2) + shape[dim + 1 :])
        bit = (me // step) % 2
        keep = lax.dynamic_index_in_dim(split, bit, axis=dim + 1, keepdims=False)
        send = lax.dynamic_index_in_dim(split, 1 - bit, axis=dim + 1, keepdims=False)
        got = lax.ppermute(send.astype(jnp.bfloat16), axis, partner(axis, step))
        blocks = keep + got.astype(jnp.float32)
        step *= 2
    return blocks


def doubling_gather(x, axis):
    me = lax.axis_index(axis)
    step = 1
    while step < lax.axis_size(axis):
        other = lax.ppermute(x, axis, partner(axis, step))
        first = (me // step) % 2 == 0
        x = jnp.where(first, jnp.concatenate([x, other]), jnp.concatenate([other, x]))
        step *= 2
    return x


def patch_matrix(slab, planes, y_cells, x_cells):
    channels = slab.shape[2]
    cells = planes * y_cells * x_cells
    shifted = jnp.stack([slab[:, :, :, dx : dx + x_cells] for dx in range(3)])

    def body(src_ref, out_ref):
        tap = pl.program_id(0)
        dz = tap // 9
        dy = (tap // 3) % 3
        dx = tap % 3
        for z in range(planes):
            for y in range(y_cells):
                out_ref[:, pl.ds((z * y_cells + y) * x_cells, x_cells)] = src_ref[dx, z + dz, y + dy]

    return pl.pallas_call(
        body,
        grid=(27,),
        in_specs=[pl.BlockSpec(shifted.shape, lambda tap: (0, 0, 0, 0, 0))],
        out_specs=pl.BlockSpec((channels, cells), lambda tap: (tap, 0)),
        out_shape=jax.ShapeDtypeStruct((27 * channels, cells), slab.dtype),
    )(shifted)


def tap_order(channels, n_taps):
    size = channels * n_taps
    new = jnp.arange(size, dtype=jnp.int32)
    old = (new % n_taps) * channels + new // n_taps
    return (old[:, None] == jnp.arange(size, dtype=jnp.int32)[None, :]).astype(jnp.bfloat16)


def block_order(n_grains, n_taps, grain):
    size = n_grains * n_taps * grain
    old = jnp.arange(size, dtype=jnp.int32)
    new = ((old // (n_taps * grain)) * grain + old % grain) * n_taps + (old // grain) % n_taps
    return (jnp.arange(size, dtype=jnp.int32)[:, None] == new[None, :]).astype(jnp.float32)


def on_device(volume, out_grad, kernel, sample_idx, a_inverse, g_inverse):
    highest = lax.Precision.HIGHEST
    f32 = jnp.float32
    channels = volume.shape[1]
    planes = volume.shape[2]
    y_cells = volume.shape[3]
    x_cells = volume.shape[4]
    cells = planes * y_cells * x_cells
    patch = kernel.shape[1]
    n_taps = patch // channels
    n_dp = lax.axis_size("dp")
    n_sp = lax.axis_size("space")
    row_ch = channels // n_dp
    col_ch = channels // n_sp
    grain = math.gcd(row_ch, col_ch)
    n_grains = channels // grain
    contract_cells = (((1,), (1,)), ((), ()))

    full_inverse = lax.all_gather(a_inverse, "space", axis=0, tiled=True)

    block = padded_2(volume, (("space", 2),), 1)
    padded = jnp.pad(block[0], ((0, 0), (0, 0), (1, 1), (1, 1)))
    slab = jnp.transpose(padded, (1, 2, 0, 3))
    patches_t = patch_matrix(slab, planes, y_cells, x_cells)
    grad_flat = out_grad[0].reshape(channels, cells)
    kernel_perm = kernel.reshape(channels, channels, n_taps).transpose(0, 2, 1).reshape(channels, patch)

    grad_perm = lax.dot_general(grad_flat, patches_t, contract_cells, preferred_element_type=f32)
    g_part = lax.dot_general(grad_flat, grad_flat, contract_cells, preferred_element_type=f32)
    terms = jnp.concatenate([grad_perm, g_part], axis=1)
    terms, patches_t = lax.optimization_barrier((terms, patches_t))
    both = butterfly_sum(terms, ("dp", "space"))
    grad_sum = (
        both[:, :patch].reshape(channels, n_taps, channels).transpose(0, 2, 1).reshape(channels, patch)
    )
    g_factor = both[:, patch:]
    left = jnp.dot(g_inverse, grad_sum, precision=highest)
    pre_grad = jnp.dot(left, full_inverse, precision=highest)

    forward = jnp.dot(kernel_perm, patches_t, preferred_element_type=f32)
    conv_out = forward.astype(jnp.bfloat16).reshape(1, channels, planes, y_cells, x_cells)

    cell_ids = sample_idx[0]
    counts = jnp.sum(
        (cell_ids[:, None] == jnp.arange(cells, dtype=jnp.int32)[None, :]).astype(f32), axis=0
    )
    weighted = patches_t.astype(f32) * counts[None, :]
    high = weighted.astype(jnp.bfloat16)
    low = (weighted - high.astype(f32)).astype(jnp.bfloat16)
    total_samples = sample_idx.shape[1] * n_sp * n_dp
    a_perm = (
        lax.dot_general(high, patches_t, contract_cells, preferred_element_type=f32)
        + lax.dot_general(low, patches_t, contract_cells, preferred_element_type=f32)
    ) / jnp.float32(total_samples)
    order = tap_order(channels, n_taps)
    a_rows = jnp.dot(order, a_perm.astype(jnp.bfloat16), preferred_element_type=f32)
    a_orig = lax.dot_general(
        a_rows.astype(jnp.bfloat16), order, contract_cells, preferred_element_type=f32
    ).astype(jnp.bfloat16)
    rows = patch // n_dp
    cols = patch // n_sp
    a_blocks = (
        a_orig.reshape(n_dp, rows, n_sp, cols).transpose(0, 2, 1, 3).reshape(n_dp * n_sp, rows, cols)
    )
    got = lax.all_to_all(a_blocks, ("dp", "space"), 0, 0, tiled=True)
    a_factor = jnp.sum(got.astype(f32), axis=0)
    return (conv_out, a_factor, g_factor, pre_grad)


def solution(mesh):
    placed = (
        P("dp", None, "space", None, None),
        P("dp", None, "space", None, None),
        P(),
        P("dp", "space"),
        P("space", None),
        P(),
    )
    return jax.shard_map(
        on_device,
        mesh=mesh,
        in_specs=placed,
        out_specs=(P("dp", None, "space", None, None), P("dp", "space"), P(), P()),
        check_vma=False,
    )
```

```python
import math

import jax
import jax.numpy as jnp
from jax import lax
from jax.experimental import pallas as pl
from jax.sharding import PartitionSpec as P


def padded_2(cells, sides, width):
    for axis, dim in sides:
        count = lax.axis_size(axis)
        ends = count - 1
        head = lax.slice_in_dim(cells, 0, width, axis=dim)
        tail = lax.slice_in_dim(cells, cells.shape[dim] - width, cells.shape[dim], axis=dim)
        cells = jnp.concatenate(
            [
                lax.ppermute(tail, axis, [(i, (i + 1) % count) for i in range(ends)]),
                cells,
                lax.ppermute(head, axis, [((i + 1) % count, i) for i in range(ends)]),
            ],
            axis=dim,
        )
    return cells


def partner(axis, step):
    return [(i, i ^ step) for i in range(lax.axis_size(axis))]


def butterfly_sum(x, axes):
    for axis in axes:
        size = lax.axis_size(axis)
        low = 1
        while low < size:
            high = low * 2
            got = lax.ppermute(x, axis, partner(axis, low))
            if high < size:
                pair = lax.ppermute(x, axis, partner(axis, high))
                other = lax.ppermute(x, axis, partner(axis, low + high))
                x = (x + got) + (pair + other)
                low = high * 2
            else:
                x = x + got
                low = high
    return x


def halving_scatter(blocks, axis, dim):
    me = lax.axis_index(axis)
    step = 1
    while step < lax.axis_size(axis):
        shape = blocks.shape
        split = blocks.reshape(shape[:dim] + (shape[dim] // 2, 2) + shape[dim + 1 :])
        bit = (me // step) % 2
        keep = lax.dynamic_index_in_dim(split, bit, axis=dim + 1, keepdims=False)
        send = lax.dynamic_index_in_dim(split, 1 - bit, axis=dim + 1, keepdims=False)
        got = lax.ppermute(send.astype(jnp.bfloat16), axis, partner(axis, step))
        blocks = keep + got.astype(jnp.float32)
        step *= 2
    return blocks


def doubling_gather(x, axis):
    me = lax.axis_index(axis)
    step = 1
    while step < lax.axis_size(axis):
        other = lax.ppermute(x, axis, partner(axis, step))
        first = (me // step) % 2 == 0
        x = jnp.where(first, jnp.concatenate([x, other]), jnp.concatenate([other, x]))
        step *= 2
    return x


def patch_matrix(slab, planes, y_cells, x_cells):
    channels = slab.shape[2]
    cells = planes * y_cells * x_cells
    shifted = jnp.stack([slab[:, :, :, dx : dx + x_cells] for dx in range(3)])

    def body(src_ref, out_ref):
        tap = pl.program_id(0)
        dz = tap // 9
        dy = (tap // 3) % 3
        dx = tap % 3
        for z in range(planes):
            for y in range(y_cells):
                out_ref[:, pl.ds((z * y_cells + y) * x_cells, x_cells)] = src_ref[dx, z + dz, y + dy]

    return pl.pallas_call(
        body,
        grid=(27,),
        in_specs=[pl.BlockSpec(shifted.shape, lambda tap: (0, 0, 0, 0, 0))],
        out_specs=pl.BlockSpec((channels, cells), lambda tap: (tap, 0)),
        out_shape=jax.ShapeDtypeStruct((27 * channels, cells), slab.dtype),
    )(shifted)


def tap_order(channels, n_taps):
    size = channels * n_taps
    new = jnp.arange(size, dtype=jnp.int32)
    old = (new % n_taps) * channels + new // n_taps
    return (old[:, None] == jnp.arange(size, dtype=jnp.int32)[None, :]).astype(jnp.bfloat16)


def block_order(n_grains, n_taps, grain):
    size = n_grains * n_taps * grain
    old = jnp.arange(size, dtype=jnp.int32)
    new = ((old // (n_taps * grain)) * grain + old % grain) * n_taps + (old // grain) % n_taps
    return (jnp.arange(size, dtype=jnp.int32)[:, None] == new[None, :]).astype(jnp.float32)


def on_device(volume, out_grad, kernel, sample_idx, a_inverse, g_inverse):
    highest = lax.Precision.HIGHEST
    f32 = jnp.float32
    channels = volume.shape[1]
    planes = volume.shape[2]
    y_cells = volume.shape[3]
    x_cells = volume.shape[4]
    cells = planes * y_cells * x_cells
    patch = kernel.shape[1]
    n_taps = patch // channels
    n_dp = lax.axis_size("dp")
    n_sp = lax.axis_size("space")
    row_ch = channels // n_dp
    col_ch = channels // n_sp
    grain = math.gcd(row_ch, col_ch)
    n_grains = channels // grain
    contract_cells = (((1,), (1,)), ((), ()))

    full_inverse = lax.all_gather(a_inverse, "space", axis=0, tiled=True)

    block = padded_2(volume, (("space", 2),), 1)
    padded = jnp.pad(block[0], ((0, 0), (0, 0), (1, 1), (1, 1)))
    slab = jnp.transpose(padded, (1, 2, 0, 3))
    patches_t = patch_matrix(slab, planes, y_cells, x_cells)
    grad_flat = out_grad[0].reshape(channels, cells)
    kernel_perm = kernel.reshape(channels, channels, n_taps).transpose(0, 2, 1).reshape(channels, patch)

    grad_perm = lax.dot_general(grad_flat, patches_t, contract_cells, preferred_element_type=f32)
    g_part = lax.dot_general(grad_flat, grad_flat, contract_cells, preferred_element_type=f32)
    terms = jnp.concatenate([grad_perm, g_part], axis=1)
    terms, patches_t = lax.optimization_barrier((terms, patches_t))
    both = butterfly_sum(terms, ("dp", "space"))
    grad_sum = (
        both[:, :patch].reshape(channels, n_taps, channels).transpose(0, 2, 1).reshape(channels, patch)
    )
    g_factor = both[:, patch:]
    left = jnp.dot(g_inverse, grad_sum, precision=highest)
    pre_grad = jnp.dot(left, full_inverse, precision=highest)

    forward = jnp.dot(kernel_perm, patches_t, preferred_element_type=f32)
    conv_out = forward.astype(jnp.bfloat16).reshape(1, channels, planes, y_cells, x_cells)

    cell_ids = sample_idx[0]
    counts = jnp.sum(
        (cell_ids[:, None] == jnp.arange(cells, dtype=jnp.int32)[None, :]).astype(f32), axis=0
    )
    weighted = patches_t.astype(f32) * counts[None, :]
    high = weighted.astype(jnp.bfloat16)
    low = (weighted - high.astype(f32)).astype(jnp.bfloat16)
    total_samples = sample_idx.shape[1] * n_sp * n_dp
    a_perm = (
        lax.dot_general(high, patches_t, contract_cells, preferred_element_type=f32)
        + lax.dot_general(low, patches_t, contract_cells, preferred_element_type=f32)
    ) / jnp.float32(total_samples)
    order = tap_order(channels, n_taps)
    a_rows = jnp.dot(order, a_perm.astype(jnp.bfloat16), preferred_element_type=f32)
    a_orig = lax.dot_general(
        a_rows.astype(jnp.bfloat16), order, contract_cells, preferred_element_type=f32
    ).astype(jnp.bfloat16)
    rows = patch // n_dp
    cols = patch // n_sp
    a_blocks = (
        a_orig.reshape(n_dp, rows, n_sp, cols).transpose(0, 2, 1, 3).reshape(n_dp * n_sp, rows, cols)
    )
    got = lax.all_to_all(a_blocks, ("dp", "space"), 0, 0, tiled=True)
    a_factor = jnp.sum(got.astype(f32), axis=0)
    return (conv_out, a_factor, g_factor, pre_grad)


def solution(mesh):
    placed = (
        P("dp", None, "space", None, None),
        P("dp", None, "space", None, None),
        P(),
        P("dp", "space"),
        P("space", None),
        P(),
    )
    return jax.shard_map(
        on_device,
        mesh=mesh,
        in_specs=placed,
        out_specs=(P("dp", None, "space", None, None), P("dp", "space"), P(), P()),
        check_vma=False,
    )
```

```python
import math

import jax
import jax.numpy as jnp
from jax import lax
from jax.experimental import pallas as pl
from jax.sharding import PartitionSpec as P


def padded_2(cells, sides, width):
    for axis, dim in sides:
        count = lax.axis_size(axis)
        ends = count - 1
        head = lax.slice_in_dim(cells, 0, width, axis=dim)
        tail = lax.slice_in_dim(cells, cells.shape[dim] - width, cells.shape[dim], axis=dim)
        cells = jnp.concatenate(
            [
                lax.ppermute(tail, axis, [(i, (i + 1) % count) for i in range(ends)]),
                cells,
                lax.ppermute(head, axis, [((i + 1) % count, i) for i in range(ends)]),
            ],
            axis=dim,
        )
    return cells


def partner(axis, step):
    return [(i, i ^ step) for i in range(lax.axis_size(axis))]


def butterfly_sum(x, axes):
    for axis in axes:
        size = lax.axis_size(axis)
        low = 1
        while low < size:
            high = low * 2
            got = lax.ppermute(x, axis, partner(axis, low))
            if high < size:
                pair = lax.ppermute(x, axis, partner(axis, high))
                other = lax.ppermute(x, axis, partner(axis, low + high))
                x = (x + got) + (pair + other)
                low = high * 2
            else:
                x = x + got
                low = high
    return x


def halving_scatter(blocks, axis, dim):
    me = lax.axis_index(axis)
    step = 1
    while step < lax.axis_size(axis):
        shape = blocks.shape
        split = blocks.reshape(shape[:dim] + (shape[dim] // 2, 2) + shape[dim + 1 :])
        bit = (me // step) % 2
        keep = lax.dynamic_index_in_dim(split, bit, axis=dim + 1, keepdims=False)
        send = lax.dynamic_index_in_dim(split, 1 - bit, axis=dim + 1, keepdims=False)
        got = lax.ppermute(send.astype(jnp.bfloat16), axis, partner(axis, step))
        blocks = keep + got.astype(jnp.float32)
        step *= 2
    return blocks


def doubling_gather(x, axis):
    me = lax.axis_index(axis)
    step = 1
    while step < lax.axis_size(axis):
        other = lax.ppermute(x, axis, partner(axis, step))
        first = (me // step) % 2 == 0
        x = jnp.where(first, jnp.concatenate([x, other]), jnp.concatenate([other, x]))
        step *= 2
    return x


def patch_matrix(slab, planes, y_cells, x_cells):
    channels = slab.shape[2]
    cells = planes * y_cells * x_cells
    shifted = jnp.stack([slab[:, :, :, dx : dx + x_cells] for dx in range(3)])

    def body(src_ref, out_ref):
        tap = pl.program_id(0)
        dz = tap // 9
        dy = (tap // 3) % 3
        dx = tap % 3
        for z in range(planes):
            for y in range(y_cells):
                out_ref[:, pl.ds((z * y_cells + y) * x_cells, x_cells)] = src_ref[dx, z + dz, y + dy]

    return pl.pallas_call(
        body,
        grid=(27,),
        in_specs=[pl.BlockSpec(shifted.shape, lambda tap: (0, 0, 0, 0, 0))],
        out_specs=pl.BlockSpec((channels, cells), lambda tap: (tap, 0)),
        out_shape=jax.ShapeDtypeStruct((27 * channels, cells), slab.dtype),
    )(shifted)


def tap_order(channels, n_taps):
    size = channels * n_taps
    new = jnp.arange(size, dtype=jnp.int32)
    old = (new % n_taps) * channels + new // n_taps
    return (old[:, None] == jnp.arange(size, dtype=jnp.int32)[None, :]).astype(jnp.bfloat16)


def block_order(n_grains, n_taps, grain):
    size = n_grains * n_taps * grain
    old = jnp.arange(size, dtype=jnp.int32)
    new = ((old // (n_taps * grain)) * grain + old % grain) * n_taps + (old // grain) % n_taps
    return (jnp.arange(size, dtype=jnp.int32)[:, None] == new[None, :]).astype(jnp.float32)


def on_device(volume, out_grad, kernel, sample_idx, a_inverse, g_inverse):
    highest = lax.Precision.HIGHEST
    f32 = jnp.float32
    channels = volume.shape[1]
    planes = volume.shape[2]
    y_cells = volume.shape[3]
    x_cells = volume.shape[4]
    cells = planes * y_cells * x_cells
    patch = kernel.shape[1]
    n_taps = patch // channels
    n_dp = lax.axis_size("dp")
    n_sp = lax.axis_size("space")
    row_ch = channels // n_dp
    col_ch = channels // n_sp
    grain = math.gcd(row_ch, col_ch)
    n_grains = channels // grain
    contract_cells = (((1,), (1,)), ((), ()))

    full_inverse = lax.all_gather(a_inverse, "space", axis=0, tiled=True)

    block = padded_2(volume, (("space", 2),), 1)
    padded = jnp.pad(block[0], ((0, 0), (0, 0), (1, 1), (1, 1)))
    slab = jnp.transpose(padded, (1, 2, 0, 3))
    patches_t = patch_matrix(slab, planes, y_cells, x_cells)
    grad_flat = out_grad[0].reshape(channels, cells)
    kernel_perm = kernel.reshape(channels, channels, n_taps).transpose(0, 2, 1).reshape(channels, patch)

    grad_perm = lax.dot_general(grad_flat, patches_t, contract_cells, preferred_element_type=f32)
    g_part = lax.dot_general(grad_flat, grad_flat, contract_cells, preferred_element_type=f32)
    terms = jnp.concatenate([grad_perm, g_part], axis=1)
    terms, patches_t = lax.optimization_barrier((terms, patches_t))
    both = butterfly_sum(terms, ("dp", "space"))
    grad_sum = (
        both[:, :patch].reshape(channels, n_taps, channels).transpose(0, 2, 1).reshape(channels, patch)
    )
    g_factor = both[:, patch:]
    left = jnp.dot(g_inverse, grad_sum, precision=highest)
    pre_grad = jnp.dot(left, full_inverse, precision=highest)

    forward = jnp.dot(kernel_perm, patches_t, preferred_element_type=f32)
    conv_out = forward.astype(jnp.bfloat16).reshape(1, channels, planes, y_cells, x_cells)

    cell_ids = sample_idx[0]
    counts = jnp.sum(
        (cell_ids[:, None] == jnp.arange(cells, dtype=jnp.int32)[None, :]).astype(f32), axis=0
    )
    weighted = patches_t.astype(f32) * counts[None, :]
    high = weighted.astype(jnp.bfloat16)
    low = (weighted - high.astype(f32)).astype(jnp.bfloat16)
    total_samples = sample_idx.shape[1] * n_sp * n_dp
    a_perm = (
        lax.dot_general(high, patches_t, contract_cells, preferred_element_type=f32)
        + lax.dot_general(low, patches_t, contract_cells, preferred_element_type=f32)
    ) / jnp.float32(total_samples)
    order = tap_order(channels, n_taps)
    a_rows = jnp.dot(order, a_perm.astype(jnp.bfloat16), preferred_element_type=f32)
    a_orig = lax.dot_general(
        a_rows.astype(jnp.bfloat16), order, contract_cells, preferred_element_type=f32
    )
    rows = patch // n_dp
    cols = patch // n_sp
    a_rows = halving_scatter(a_orig.reshape(n_dp, rows, patch), "dp", 0)
    a_factor = halving_scatter(a_rows.reshape(rows, n_sp, cols), "space", 1).reshape(rows, cols)
    return (conv_out, a_factor, g_factor, pre_grad)


def solution(mesh):
    placed = (
        P("dp", None, "space", None, None),
        P("dp", None, "space", None, None),
        P(),
        P("dp", "space"),
        P("space", None),
        P(),
    )
    return jax.shard_map(
        on_device,
        mesh=mesh,
        in_specs=placed,
        out_specs=(P("dp", None, "space", None, None), P("dp", "space"), P(), P()),
        check_vma=False,
    )
```

```python
import math

import jax
import jax.numpy as jnp
from jax import lax
from jax.experimental import pallas as pl
from jax.sharding import PartitionSpec as P


def padded_2(cells, sides, width):
    for axis, dim in sides:
        count = lax.axis_size(axis)
        ends = count - 1
        head = lax.slice_in_dim(cells, 0, width, axis=dim)
        tail = lax.slice_in_dim(cells, cells.shape[dim] - width, cells.shape[dim], axis=dim)
        cells = jnp.concatenate(
            [
                lax.ppermute(tail, axis, [(i, (i + 1) % count) for i in range(ends)]),
                cells,
                lax.ppermute(head, axis, [((i + 1) % count, i) for i in range(ends)]),
            ],
            axis=dim,
        )
    return cells


def partner(axis, step):
    return [(i, i ^ step) for i in range(lax.axis_size(axis))]


def butterfly_sum(x, axes):
    for axis in axes:
        size = lax.axis_size(axis)
        low = 1
        while low < size:
            high = low * 2
            got = lax.ppermute(x, axis, partner(axis, low))
            if high < size:
                pair = lax.ppermute(x, axis, partner(axis, high))
                other = lax.ppermute(x, axis, partner(axis, low + high))
                x = (x + got) + (pair + other)
                low = high * 2
            else:
                x = x + got
                low = high
    return x


def halving_scatter(blocks, axis, dim, wire=jnp.bfloat16):
    me = lax.axis_index(axis)
    step = 1
    while step < lax.axis_size(axis):
        shape = blocks.shape
        split = blocks.reshape(shape[:dim] + (shape[dim] // 2, 2) + shape[dim + 1 :])
        bit = (me // step) % 2
        keep = lax.dynamic_index_in_dim(split, bit, axis=dim + 1, keepdims=False)
        send = lax.dynamic_index_in_dim(split, 1 - bit, axis=dim + 1, keepdims=False)
        got = lax.ppermute(send.astype(wire), axis, partner(axis, step))
        blocks = keep + got.astype(jnp.float32)
        step *= 2
    return blocks


def doubling_gather(x, axis):
    me = lax.axis_index(axis)
    step = 1
    while step < lax.axis_size(axis):
        other = lax.ppermute(x, axis, partner(axis, step))
        first = (me // step) % 2 == 0
        x = jnp.where(first, jnp.concatenate([x, other]), jnp.concatenate([other, x]))
        step *= 2
    return x


def patch_matrix(slab, planes, y_cells, x_cells):
    channels = slab.shape[2]
    cells = planes * y_cells * x_cells
    shifted = jnp.stack([slab[:, :, :, dx : dx + x_cells] for dx in range(3)])

    def body(src_ref, out_ref):
        tap = pl.program_id(0)
        dz = tap // 9
        dy = (tap // 3) % 3
        dx = tap % 3
        for z in range(planes):
            for y in range(y_cells):
                out_ref[:, pl.ds((z * y_cells + y) * x_cells, x_cells)] = src_ref[dx, z + dz, y + dy]

    return pl.pallas_call(
        body,
        grid=(27,),
        in_specs=[pl.BlockSpec(shifted.shape, lambda tap: (0, 0, 0, 0, 0))],
        out_specs=pl.BlockSpec((channels, cells), lambda tap: (tap, 0)),
        out_shape=jax.ShapeDtypeStruct((27 * channels, cells), slab.dtype),
    )(shifted)


def tap_order(channels, n_taps):
    size = channels * n_taps
    new = jnp.arange(size, dtype=jnp.int32)
    old = (new % n_taps) * channels + new // n_taps
    return (old[:, None] == jnp.arange(size, dtype=jnp.int32)[None, :]).astype(jnp.bfloat16)


def block_order(n_grains, n_taps, grain):
    size = n_grains * n_taps * grain
    old = jnp.arange(size, dtype=jnp.int32)
    new = ((old // (n_taps * grain)) * grain + old % grain) * n_taps + (old // grain) % n_taps
    return (jnp.arange(size, dtype=jnp.int32)[:, None] == new[None, :]).astype(jnp.float32)


def on_device(volume, out_grad, kernel, sample_idx, a_inverse, g_inverse):
    highest = lax.Precision.HIGHEST
    f32 = jnp.float32
    channels = volume.shape[1]
    planes = volume.shape[2]
    y_cells = volume.shape[3]
    x_cells = volume.shape[4]
    cells = planes * y_cells * x_cells
    patch = kernel.shape[1]
    n_taps = patch // channels
    n_dp = lax.axis_size("dp")
    n_sp = lax.axis_size("space")
    row_ch = channels // n_dp
    col_ch = channels // n_sp
    grain = math.gcd(row_ch, col_ch)
    n_grains = channels // grain
    contract_cells = (((1,), (1,)), ((), ()))

    block = padded_2(volume, (("space", 2),), 1)
    padded = jnp.pad(block[0], ((0, 0), (0, 0), (1, 1), (1, 1)))
    slab = jnp.transpose(padded, (1, 2, 0, 3))
    patches_t = patch_matrix(slab, planes, y_cells, x_cells)
    grad_flat = out_grad[0].reshape(channels, cells)
    kernel_perm = kernel.reshape(channels, channels, n_taps).transpose(0, 2, 1).reshape(channels, patch)

    grad_perm = lax.dot_general(grad_flat, patches_t, contract_cells, preferred_element_type=f32)
    g_part = lax.dot_general(grad_flat, grad_flat, contract_cells, preferred_element_type=f32)
    terms = jnp.concatenate([grad_perm, g_part], axis=1)
    terms, patches_t = lax.optimization_barrier((terms, patches_t))
    plane = butterfly_sum(terms, ("dp",))
    grad_plane = (
        plane[:, :patch].reshape(channels, n_taps, channels).transpose(0, 2, 1).reshape(channels, patch)
    )
    own_cols = halving_scatter(
        grad_plane.reshape(channels, n_sp, patch // n_sp), "space", 1, wire=f32
    ).reshape(channels, patch // n_sp)
    left = jnp.dot(g_inverse, own_cols, precision=highest)
    partial = jnp.dot(left, a_inverse, precision=highest)
    both = butterfly_sum(jnp.concatenate([partial, plane[:, patch:]], axis=1), ("space",))
    pre_grad = both[:, :patch]
    g_factor = both[:, patch:]

    forward = jnp.dot(kernel_perm, patches_t, preferred_element_type=f32)
    conv_out = forward.astype(jnp.bfloat16).reshape(1, channels, planes, y_cells, x_cells)

    cell_ids = sample_idx[0]
    counts = jnp.sum(
        (cell_ids[:, None] == jnp.arange(cells, dtype=jnp.int32)[None, :]).astype(f32), axis=0
    )
    weighted = patches_t.astype(f32) * counts[None, :]
    high = weighted.astype(jnp.bfloat16)
    low = (weighted - high.astype(f32)).astype(jnp.bfloat16)
    total_samples = sample_idx.shape[1] * n_sp * n_dp
    a_perm = (
        lax.dot_general(high, patches_t, contract_cells, preferred_element_type=f32)
        + lax.dot_general(low, patches_t, contract_cells, preferred_element_type=f32)
    ) / jnp.float32(total_samples)
    order = tap_order(channels, n_taps)
    a_rows = jnp.dot(order, a_perm.astype(jnp.bfloat16), preferred_element_type=f32)
    a_orig = lax.dot_general(
        a_rows.astype(jnp.bfloat16), order, contract_cells, preferred_element_type=f32
    )
    rows = patch // n_dp
    cols = patch // n_sp
    a_rows = halving_scatter(a_orig.reshape(n_dp, rows, patch), "dp", 0)
    a_factor = halving_scatter(a_rows.reshape(rows, n_sp, cols), "space", 1).reshape(rows, cols)
    return (conv_out, a_factor, g_factor, pre_grad)


def solution(mesh):
    placed = (
        P("dp", None, "space", None, None),
        P("dp", None, "space", None, None),
        P(),
        P("dp", "space"),
        P("space", None),
        P(),
    )
    return jax.shard_map(
        on_device,
        mesh=mesh,
        in_specs=placed,
        out_specs=(P("dp", None, "space", None, None), P("dp", "space"), P(), P()),
        check_vma=False,
    )
```

```python
import math

import jax
import jax.numpy as jnp
from jax import lax
from jax.experimental import pallas as pl
from jax.sharding import PartitionSpec as P


def padded_2(cells, sides, width):
    for axis, dim in sides:
        count = lax.axis_size(axis)
        ends = count - 1
        head = lax.slice_in_dim(cells, 0, width, axis=dim)
        tail = lax.slice_in_dim(cells, cells.shape[dim] - width, cells.shape[dim], axis=dim)
        cells = jnp.concatenate(
            [
                lax.ppermute(tail, axis, [(i, (i + 1) % count) for i in range(ends)]),
                cells,
                lax.ppermute(head, axis, [((i + 1) % count, i) for i in range(ends)]),
            ],
            axis=dim,
        )
    return cells


def partner(axis, step):
    return [(i, i ^ step) for i in range(lax.axis_size(axis))]


def butterfly_sum(x, axes):
    for axis in axes:
        size = lax.axis_size(axis)
        low = 1
        while low < size:
            high = low * 2
            got = lax.ppermute(x, axis, partner(axis, low))
            if high < size:
                pair = lax.ppermute(x, axis, partner(axis, high))
                other = lax.ppermute(x, axis, partner(axis, low + high))
                x = (x + got) + (pair + other)
                low = high * 2
            else:
                x = x + got
                low = high
    return x


def halving_scatter(blocks, axis, dim, wire=jnp.bfloat16):
    me = lax.axis_index(axis)
    step = 1
    while step < lax.axis_size(axis):
        shape = blocks.shape
        split = blocks.reshape(shape[:dim] + (shape[dim] // 2, 2) + shape[dim + 1 :])
        bit = (me // step) % 2
        keep = lax.dynamic_index_in_dim(split, bit, axis=dim + 1, keepdims=False)
        send = lax.dynamic_index_in_dim(split, 1 - bit, axis=dim + 1, keepdims=False)
        got = lax.ppermute(send.astype(wire), axis, partner(axis, step))
        blocks = keep + got.astype(jnp.float32)
        step *= 2
    return blocks


def doubling_gather(x, axis):
    me = lax.axis_index(axis)
    step = 1
    while step < lax.axis_size(axis):
        other = lax.ppermute(x, axis, partner(axis, step))
        first = (me // step) % 2 == 0
        x = jnp.where(first, jnp.concatenate([x, other]), jnp.concatenate([other, x]))
        step *= 2
    return x


def patch_matrix(slab, planes, y_cells, x_cells):
    channels = slab.shape[2]
    cells = planes * y_cells * x_cells
    shifted = jnp.stack([slab[:, :, :, dx : dx + x_cells] for dx in range(3)])

    def body(src_ref, out_ref):
        dz = pl.program_id(0)
        for dy in range(3):
            for dx in range(3):
                row = (dy * 3 + dx) * channels
                for z in range(planes):
                    for y in range(y_cells):
                        out_ref[pl.ds(row, channels), pl.ds((z * y_cells + y) * x_cells, x_cells)] = (
                            src_ref[dx, z + dz, y + dy]
                        )

    return pl.pallas_call(
        body,
        grid=(3,),
        in_specs=[pl.BlockSpec(shifted.shape, lambda dz: (0, 0, 0, 0, 0))],
        out_specs=pl.BlockSpec((9 * channels, cells), lambda dz: (dz, 0)),
        out_shape=jax.ShapeDtypeStruct((27 * channels, cells), slab.dtype),
    )(shifted)


def tap_order(channels, n_taps):
    size = channels * n_taps
    new = jnp.arange(size, dtype=jnp.int32)
    old = (new % n_taps) * channels + new // n_taps
    return (old[:, None] == jnp.arange(size, dtype=jnp.int32)[None, :]).astype(jnp.bfloat16)


def block_order(n_grains, n_taps, grain):
    size = n_grains * n_taps * grain
    old = jnp.arange(size, dtype=jnp.int32)
    new = ((old // (n_taps * grain)) * grain + old % grain) * n_taps + (old // grain) % n_taps
    return (jnp.arange(size, dtype=jnp.int32)[:, None] == new[None, :]).astype(jnp.float32)


def on_device(volume, out_grad, kernel, sample_idx, a_inverse, g_inverse):
    highest = lax.Precision.HIGHEST
    f32 = jnp.float32
    channels = volume.shape[1]
    planes = volume.shape[2]
    y_cells = volume.shape[3]
    x_cells = volume.shape[4]
    cells = planes * y_cells * x_cells
    patch = kernel.shape[1]
    n_taps = patch // channels
    n_dp = lax.axis_size("dp")
    n_sp = lax.axis_size("space")
    row_ch = channels // n_dp
    col_ch = channels // n_sp
    grain = math.gcd(row_ch, col_ch)
    n_grains = channels // grain
    contract_cells = (((1,), (1,)), ((), ()))

    block = padded_2(volume, (("space", 2),), 1)
    padded = jnp.pad(block[0], ((0, 0), (0, 0), (1, 1), (1, 1)))
    slab = jnp.transpose(padded, (1, 2, 0, 3))
    patches_t = patch_matrix(slab, planes, y_cells, x_cells)
    grad_flat = out_grad[0].reshape(channels, cells)
    kernel_perm = kernel.reshape(channels, channels, n_taps).transpose(0, 2, 1).reshape(channels, patch)

    grad_perm = lax.dot_general(grad_flat, patches_t, contract_cells, preferred_element_type=f32)
    g_part = lax.dot_general(grad_flat, grad_flat, contract_cells, preferred_element_type=f32)
    terms = jnp.concatenate([grad_perm, g_part], axis=1)
    terms, patches_t = lax.optimization_barrier((terms, patches_t))
    plane = butterfly_sum(terms, ("dp",))
    grad_plane = (
        plane[:, :patch].reshape(channels, n_taps, channels).transpose(0, 2, 1).reshape(channels, patch)
    )
    own_cols = halving_scatter(
        grad_plane.reshape(channels, n_sp, patch // n_sp), "space", 1, wire=f32
    ).reshape(channels, patch // n_sp)
    left = jnp.dot(g_inverse, own_cols, precision=highest)
    partial = jnp.dot(left, a_inverse, precision=highest)
    both = butterfly_sum(jnp.concatenate([partial, plane[:, patch:]], axis=1), ("space",))
    pre_grad = both[:, :patch]
    g_factor = both[:, patch:]


    cell_ids = sample_idx[0]
    counts = jnp.sum(
        (cell_ids[:, None] == jnp.arange(cells, dtype=jnp.int32)[None, :]).astype(f32), axis=0
    )
    weighted = (patches_t.astype(f32) * counts[None, :]).astype(jnp.bfloat16)
    total_samples = sample_idx.shape[1] * n_sp * n_dp
    a_perm = lax.dot_general(
        weighted, patches_t, contract_cells, preferred_element_type=f32
    ) / jnp.float32(total_samples)
    order = tap_order(channels, n_taps)
    a_rows = jnp.dot(order, a_perm.astype(jnp.bfloat16), preferred_element_type=f32)
    a_orig = lax.dot_general(
        a_rows.astype(jnp.bfloat16), order, contract_cells, preferred_element_type=f32
    )
    a_orig, kernel_perm = lax.optimization_barrier((a_orig, kernel_perm))
    forward = jnp.dot(kernel_perm, patches_t, preferred_element_type=f32)
    conv_out = forward.astype(jnp.bfloat16).reshape(1, channels, planes, y_cells, x_cells)
    rows = patch // n_dp
    cols = patch // n_sp
    a_rows = halving_scatter(a_orig.reshape(n_dp, rows, patch), "dp", 0)
    a_factor = halving_scatter(a_rows.reshape(rows, n_sp, cols), "space", 1).reshape(rows, cols)
    return (conv_out, a_factor, g_factor, pre_grad)


def solution(mesh):
    placed = (
        P("dp", None, "space", None, None),
        P("dp", None, "space", None, None),
        P(),
        P("dp", "space"),
        P("space", None),
        P(),
    )
    return jax.shard_map(
        on_device,
        mesh=mesh,
        in_specs=placed,
        out_specs=(P("dp", None, "space", None, None), P("dp", "space"), P(), P()),
        check_vma=False,
    )
```

```python
import math

import jax
import jax.numpy as jnp
from jax import lax
from jax.experimental import pallas as pl
from jax.sharding import PartitionSpec as P


def padded_2(cells, sides, width):
    for axis, dim in sides:
        count = lax.axis_size(axis)
        ends = count - 1
        head = lax.slice_in_dim(cells, 0, width, axis=dim)
        tail = lax.slice_in_dim(cells, cells.shape[dim] - width, cells.shape[dim], axis=dim)
        cells = jnp.concatenate(
            [
                lax.ppermute(tail, axis, [(i, (i + 1) % count) for i in range(ends)]),
                cells,
                lax.ppermute(head, axis, [((i + 1) % count, i) for i in range(ends)]),
            ],
            axis=dim,
        )
    return cells


def partner(axis, step):
    return [(i, i ^ step) for i in range(lax.axis_size(axis))]


def butterfly_sum(x, axes):
    for axis in axes:
        size = lax.axis_size(axis)
        low = 1
        while low < size:
            high = low * 2
            got = lax.ppermute(x, axis, partner(axis, low))
            if high < size:
                pair = lax.ppermute(x, axis, partner(axis, high))
                other = lax.ppermute(x, axis, partner(axis, low + high))
                x = (x + got) + (pair + other)
                low = high * 2
            else:
                x = x + got
                low = high
    return x


def halving_scatter(blocks, axis, dim, wire=jnp.bfloat16):
    me = lax.axis_index(axis)
    step = 1
    while step < lax.axis_size(axis):
        shape = blocks.shape
        split = blocks.reshape(shape[:dim] + (shape[dim] // 2, 2) + shape[dim + 1 :])
        bit = (me // step) % 2
        keep = lax.dynamic_index_in_dim(split, bit, axis=dim + 1, keepdims=False)
        send = lax.dynamic_index_in_dim(split, 1 - bit, axis=dim + 1, keepdims=False)
        got = lax.ppermute(send.astype(wire), axis, partner(axis, step))
        blocks = keep + got.astype(jnp.float32)
        step *= 2
    return blocks


def doubling_gather(x, axis):
    me = lax.axis_index(axis)
    step = 1
    while step < lax.axis_size(axis):
        other = lax.ppermute(x, axis, partner(axis, step))
        first = (me // step) % 2 == 0
        x = jnp.where(first, jnp.concatenate([x, other]), jnp.concatenate([other, x]))
        step *= 2
    return x


def patch_matrix(slab, planes, y_cells, x_cells):
    channels = slab.shape[2]
    cells = planes * y_cells * x_cells
    shifted = jnp.stack([slab[:, :, :, dx : dx + x_cells] for dx in range(3)])

    def body(src_ref, out_ref):
        dz = pl.program_id(0)
        for dy in range(3):
            for dx in range(3):
                row = (dy * 3 + dx) * channels
                for z in range(planes):
                    for y in range(y_cells):
                        out_ref[pl.ds(row, channels), pl.ds((z * y_cells + y) * x_cells, x_cells)] = (
                            src_ref[dx, z + dz, y + dy]
                        )

    return pl.pallas_call(
        body,
        grid=(3,),
        in_specs=[pl.BlockSpec(shifted.shape, lambda dz: (0, 0, 0, 0, 0))],
        out_specs=pl.BlockSpec((9 * channels, cells), lambda dz: (dz, 0)),
        out_shape=jax.ShapeDtypeStruct((27 * channels, cells), slab.dtype),
    )(shifted)


def tap_order(channels, n_taps):
    size = channels * n_taps
    new = jnp.arange(size, dtype=jnp.int32)
    old = (new % n_taps) * channels + new // n_taps
    return (old[:, None] == jnp.arange(size, dtype=jnp.int32)[None, :]).astype(jnp.bfloat16)


def block_order(n_grains, n_taps, grain):
    size = n_grains * n_taps * grain
    old = jnp.arange(size, dtype=jnp.int32)
    new = ((old // (n_taps * grain)) * grain + old % grain) * n_taps + (old // grain) % n_taps
    return (jnp.arange(size, dtype=jnp.int32)[:, None] == new[None, :]).astype(jnp.float32)


def on_device(volume, out_grad, kernel, sample_idx, a_inverse, g_inverse):
    highest = lax.Precision.HIGHEST
    f32 = jnp.float32
    channels = volume.shape[1]
    planes = volume.shape[2]
    y_cells = volume.shape[3]
    x_cells = volume.shape[4]
    cells = planes * y_cells * x_cells
    patch = kernel.shape[1]
    n_taps = patch // channels
    n_dp = lax.axis_size("dp")
    n_sp = lax.axis_size("space")
    row_ch = channels // n_dp
    col_ch = channels // n_sp
    grain = math.gcd(row_ch, col_ch)
    n_grains = channels // grain
    contract_cells = (((1,), (1,)), ((), ()))

    block = padded_2(volume, (("space", 2),), 1)
    padded = jnp.pad(block[0], ((0, 0), (0, 0), (1, 1), (1, 1)))
    slab = jnp.transpose(padded, (1, 2, 0, 3))
    patches_t = patch_matrix(slab, planes, y_cells, x_cells)
    grad_flat = out_grad[0].reshape(channels, cells)
    kernel_perm = kernel.reshape(channels, channels, n_taps).transpose(0, 2, 1).reshape(channels, patch)

    grad_perm = lax.dot_general(grad_flat, patches_t, contract_cells, preferred_element_type=f32)
    g_part = lax.dot_general(grad_flat, grad_flat, contract_cells, preferred_element_type=f32)
    terms = jnp.concatenate([grad_perm, g_part], axis=1)
    terms, patches_t = lax.optimization_barrier((terms, patches_t))
    plane = butterfly_sum(terms, ("dp",))
    grad_plane = (
        plane[:, :patch].reshape(channels, n_taps, channels).transpose(0, 2, 1).reshape(channels, patch)
    )
    own_cols = halving_scatter(
        grad_plane.reshape(channels, n_sp, patch // n_sp), "space", 1, wire=f32
    ).reshape(channels, patch // n_sp)
    left = jnp.dot(g_inverse, own_cols, precision=highest)
    partial = jnp.dot(left, a_inverse, precision=highest)
    both = butterfly_sum(jnp.concatenate([partial, plane[:, patch:]], axis=1), ("space",))
    pre_grad = both[:, :patch]
    g_factor = both[:, patch:]


    cell_ids = sample_idx[0]
    counts = jnp.sum(
        (cell_ids[:, None] == jnp.arange(cells, dtype=jnp.int32)[None, :]).astype(f32), axis=0
    )
    weighted = (patches_t.astype(f32) * counts[None, :]).astype(jnp.bfloat16)
    total_samples = sample_idx.shape[1] * n_sp * n_dp
    a_perm = lax.dot_general(
        weighted, patches_t, contract_cells, preferred_element_type=f32
    ) / jnp.float32(total_samples)
    order, a_bf = lax.optimization_barrier((tap_order(channels, n_taps), a_perm.astype(jnp.bfloat16)))
    a_rows = jnp.dot(order, a_bf, preferred_element_type=f32)
    a_orig = lax.dot_general(
        a_rows.astype(jnp.bfloat16), order, contract_cells, preferred_element_type=f32
    )
    a_orig, kernel_perm = lax.optimization_barrier((a_orig, kernel_perm))
    forward = jnp.dot(kernel_perm, patches_t, preferred_element_type=f32)
    conv_out = forward.astype(jnp.bfloat16).reshape(1, channels, planes, y_cells, x_cells)
    rows = patch // n_dp
    cols = patch // n_sp
    a_rows = halving_scatter(a_orig.reshape(n_dp, rows, patch), "dp", 0)
    a_factor = halving_scatter(a_rows.reshape(rows, n_sp, cols), "space", 1).reshape(rows, cols)
    return (conv_out, a_factor, g_factor, pre_grad)


def solution(mesh):
    placed = (
        P("dp", None, "space", None, None),
        P("dp", None, "space", None, None),
        P(),
        P("dp", "space"),
        P("space", None),
        P(),
    )
    return jax.shard_map(
        on_device,
        mesh=mesh,
        in_specs=placed,
        out_specs=(P("dp", None, "space", None, None), P("dp", "space"), P(), P()),
        check_vma=False,
    )
```

```python
import math

import jax
import jax.numpy as jnp
from jax import lax
from jax.experimental import pallas as pl
from jax.sharding import PartitionSpec as P


def padded_2(cells, sides, width):
    for axis, dim in sides:
        count = lax.axis_size(axis)
        ends = count - 1
        head = lax.slice_in_dim(cells, 0, width, axis=dim)
        tail = lax.slice_in_dim(cells, cells.shape[dim] - width, cells.shape[dim], axis=dim)
        cells = jnp.concatenate(
            [
                lax.ppermute(tail, axis, [(i, (i + 1) % count) for i in range(ends)]),
                cells,
                lax.ppermute(head, axis, [((i + 1) % count, i) for i in range(ends)]),
            ],
            axis=dim,
        )
    return cells


def partner(axis, step):
    return [(i, i ^ step) for i in range(lax.axis_size(axis))]


def butterfly_sum(x, axes):
    for axis in axes:
        size = lax.axis_size(axis)
        low = 1
        while low < size:
            high = low * 2
            got = lax.ppermute(x, axis, partner(axis, low))
            if high < size:
                pair = lax.ppermute(x, axis, partner(axis, high))
                other = lax.ppermute(x, axis, partner(axis, low + high))
                x = (x + got) + (pair + other)
                low = high * 2
            else:
                x = x + got
                low = high
    return x


def halving_scatter(blocks, axis, dim, wire=jnp.bfloat16):
    me = lax.axis_index(axis)
    step = 1
    while step < lax.axis_size(axis):
        shape = blocks.shape
        split = blocks.reshape(shape[:dim] + (shape[dim] // 2, 2) + shape[dim + 1 :])
        bit = (me // step) % 2
        keep = lax.dynamic_index_in_dim(split, bit, axis=dim + 1, keepdims=False)
        send = lax.dynamic_index_in_dim(split, 1 - bit, axis=dim + 1, keepdims=False)
        got = lax.ppermute(send.astype(wire), axis, partner(axis, step))
        blocks = keep + got.astype(jnp.float32)
        step *= 2
    return blocks


def doubling_gather(x, axis):
    me = lax.axis_index(axis)
    step = 1
    while step < lax.axis_size(axis):
        other = lax.ppermute(x, axis, partner(axis, step))
        first = (me // step) % 2 == 0
        x = jnp.where(first, jnp.concatenate([x, other]), jnp.concatenate([other, x]))
        step *= 2
    return x


def patch_matrix(slab, planes, y_cells, x_cells):
    channels = slab.shape[2]
    cells = planes * y_cells * x_cells
    shifted = jnp.stack([slab[:, :, :, dx : dx + x_cells] for dx in range(3)])

    def body(src_ref, out_ref):
        dz = pl.program_id(0)
        for dy in range(3):
            for dx in range(3):
                row = (dy * 3 + dx) * channels
                for z in range(planes):
                    for y in range(y_cells):
                        out_ref[pl.ds(row, channels), pl.ds((z * y_cells + y) * x_cells, x_cells)] = (
                            src_ref[dx, z + dz, y + dy]
                        )

    return pl.pallas_call(
        body,
        grid=(3,),
        in_specs=[pl.BlockSpec(shifted.shape, lambda dz: (0, 0, 0, 0, 0))],
        out_specs=pl.BlockSpec((9 * channels, cells), lambda dz: (dz, 0)),
        out_shape=jax.ShapeDtypeStruct((27 * channels, cells), slab.dtype),
    )(shifted)


def tap_order(channels, n_taps):
    size = channels * n_taps
    new = jnp.arange(size, dtype=jnp.int32)
    old = (new % n_taps) * channels + new // n_taps
    return (old[:, None] == jnp.arange(size, dtype=jnp.int32)[None, :]).astype(jnp.bfloat16)


def halving_order(channels, n_taps, rows, axis):
    size = channels * n_taps
    bits = lax.axis_size(axis).bit_length() - 1
    spot = jnp.arange(size, dtype=jnp.int32)
    rank = spot // rows
    flipped = sum(((rank >> b) & 1) << (bits - 1 - b) for b in range(bits))
    block = jnp.bitwise_xor(flipped, lax.axis_index(axis))
    original = block * rows + spot % rows
    source = (original % n_taps) * channels + original // n_taps
    return (source[:, None] == jnp.arange(size, dtype=jnp.int32)[None, :]).astype(jnp.bfloat16)


def block_order(n_grains, n_taps, grain):
    size = n_grains * n_taps * grain
    old = jnp.arange(size, dtype=jnp.int32)
    new = ((old // (n_taps * grain)) * grain + old % grain) * n_taps + (old // grain) % n_taps
    return (jnp.arange(size, dtype=jnp.int32)[:, None] == new[None, :]).astype(jnp.float32)


def on_device(volume, out_grad, kernel, sample_idx, a_inverse, g_inverse):
    highest = lax.Precision.HIGHEST
    f32 = jnp.float32
    channels = volume.shape[1]
    planes = volume.shape[2]
    y_cells = volume.shape[3]
    x_cells = volume.shape[4]
    cells = planes * y_cells * x_cells
    patch = kernel.shape[1]
    n_taps = patch // channels
    n_dp = lax.axis_size("dp")
    n_sp = lax.axis_size("space")
    row_ch = channels // n_dp
    col_ch = channels // n_sp
    grain = math.gcd(row_ch, col_ch)
    n_grains = channels // grain
    contract_cells = (((1,), (1,)), ((), ()))

    block = padded_2(volume, (("space", 2),), 1)
    padded = jnp.pad(block[0], ((0, 0), (0, 0), (1, 1), (1, 1)))
    slab = jnp.transpose(padded, (1, 2, 0, 3))
    patches_t = patch_matrix(slab, planes, y_cells, x_cells)
    grad_flat = out_grad[0].reshape(channels, cells)
    kernel_perm = kernel.reshape(channels, channels, n_taps).transpose(0, 2, 1).reshape(channels, patch)

    grad_perm = lax.dot_general(grad_flat, patches_t, contract_cells, preferred_element_type=f32)
    g_part = lax.dot_general(grad_flat, grad_flat, contract_cells, preferred_element_type=f32)
    terms = jnp.concatenate([grad_perm, g_part], axis=1)
    terms, patches_t = lax.optimization_barrier((terms, patches_t))
    plane = butterfly_sum(terms, ("dp",))
    grad_plane = (
        plane[:, :patch].reshape(channels, n_taps, channels).transpose(0, 2, 1).reshape(channels, patch)
    )
    own_cols = halving_scatter(
        grad_plane.reshape(channels, n_sp, patch // n_sp), "space", 1, wire=f32
    ).reshape(channels, patch // n_sp)
    left = jnp.dot(g_inverse, own_cols, precision=highest)
    partial = jnp.dot(left, a_inverse, precision=highest)
    both = butterfly_sum(jnp.concatenate([partial, plane[:, patch:]], axis=1), ("space",))
    pre_grad = both[:, :patch]
    g_factor = both[:, patch:]


    cell_ids = sample_idx[0]
    counts = jnp.sum(
        (cell_ids[:, None] == jnp.arange(cells, dtype=jnp.int32)[None, :]).astype(f32), axis=0
    )
    weighted = (patches_t.astype(f32) * counts[None, :]).astype(jnp.bfloat16)
    total_samples = sample_idx.shape[1] * n_sp * n_dp
    a_perm = lax.dot_general(
        weighted, patches_t, contract_cells, preferred_element_type=f32
    ) / jnp.float32(total_samples)
    rows = patch // n_dp
    cols = patch // n_sp
    order, placed, a_bf = lax.optimization_barrier(
        (tap_order(channels, n_taps), halving_order(channels, n_taps, rows, "dp"), a_perm.astype(jnp.bfloat16))
    )
    a_rows = jnp.dot(placed, a_bf, preferred_element_type=f32)
    a_orig, kernel_perm = lax.optimization_barrier((a_rows, kernel_perm))
    forward = jnp.dot(kernel_perm, patches_t, preferred_element_type=f32)
    conv_out = forward.astype(jnp.bfloat16).reshape(1, channels, planes, y_cells, x_cells)
    step = 1
    while step < n_dp:
        half = a_orig.shape[0] // 2
        got = lax.ppermute(a_orig[half:].astype(jnp.bfloat16), "dp", partner("dp", step))
        a_orig = a_orig[:half] + got.astype(f32)
        step *= 2
    a_block = lax.dot_general(
        a_orig, order.astype(f32), contract_cells, precision=lax.Precision.HIGH
    )
    a_factor = halving_scatter(a_block.reshape(rows, n_sp, cols), "space", 1).reshape(rows, cols)
    return (conv_out, a_factor, g_factor, pre_grad)


def solution(mesh):
    placed = (
        P("dp", None, "space", None, None),
        P("dp", None, "space", None, None),
        P(),
        P("dp", "space"),
        P("space", None),
        P(),
    )
    return jax.shard_map(
        on_device,
        mesh=mesh,
        in_specs=placed,
        out_specs=(P("dp", None, "space", None, None), P("dp", "space"), P(), P()),
        check_vma=False,
    )
```

```python
import math

import jax
import jax.numpy as jnp
from jax import lax
from jax.experimental import pallas as pl
from jax.sharding import PartitionSpec as P


def padded_2(cells, sides, width):
    for axis, dim in sides:
        count = lax.axis_size(axis)
        ends = count - 1
        head = lax.slice_in_dim(cells, 0, width, axis=dim)
        tail = lax.slice_in_dim(cells, cells.shape[dim] - width, cells.shape[dim], axis=dim)
        cells = jnp.concatenate(
            [
                lax.ppermute(tail, axis, [(i, (i + 1) % count) for i in range(ends)]),
                cells,
                lax.ppermute(head, axis, [((i + 1) % count, i) for i in range(ends)]),
            ],
            axis=dim,
        )
    return cells


def partner(axis, step):
    return [(i, i ^ step) for i in range(lax.axis_size(axis))]


def butterfly_sum(x, axes):
    for axis in axes:
        size = lax.axis_size(axis)
        low = 1
        while low < size:
            high = low * 2
            got = lax.ppermute(x, axis, partner(axis, low))
            if high < size:
                pair = lax.ppermute(x, axis, partner(axis, high))
                other = lax.ppermute(x, axis, partner(axis, low + high))
                x = (x + got) + (pair + other)
                low = high * 2
            else:
                x = x + got
                low = high
    return x


def halving_scatter(blocks, axis, dim, wire=jnp.bfloat16):
    me = lax.axis_index(axis)
    step = 1
    while step < lax.axis_size(axis):
        shape = blocks.shape
        split = blocks.reshape(shape[:dim] + (shape[dim] // 2, 2) + shape[dim + 1 :])
        bit = (me // step) % 2
        keep = lax.dynamic_index_in_dim(split, bit, axis=dim + 1, keepdims=False)
        send = lax.dynamic_index_in_dim(split, 1 - bit, axis=dim + 1, keepdims=False)
        got = lax.ppermute(send.astype(wire), axis, partner(axis, step))
        blocks = keep + got.astype(jnp.float32)
        step *= 2
    return blocks


def quad_scatter(blocks, axis, dim):
    me = lax.axis_index(axis)
    low = 1
    while low < lax.axis_size(axis):
        shape = blocks.shape
        if low * 2 < lax.axis_size(axis):
            split = blocks.reshape(shape[:dim] + (shape[dim] // 4, 4) + shape[dim + 1 :])
            digit = (me // low) % 4

            def pick(d):
                return lax.dynamic_index_in_dim(split, d, axis=dim + 1, keepdims=False)

            got = [
                lax.ppermute(pick(digit ^ k).astype(jnp.bfloat16), axis, partner(axis, k * low)).astype(
                    jnp.float32
                )
                for k in (1, 2, 3)
            ]
            blocks = (pick(digit) + got[0]) + (got[1] + got[2])
            low *= 4
        else:
            split = blocks.reshape(shape[:dim] + (shape[dim] // 2, 2) + shape[dim + 1 :])
            bit = (me // low) % 2
            keep = lax.dynamic_index_in_dim(split, bit, axis=dim + 1, keepdims=False)
            send = lax.dynamic_index_in_dim(split, 1 - bit, axis=dim + 1, keepdims=False)
            got = lax.ppermute(send.astype(jnp.bfloat16), axis, partner(axis, low))
            blocks = keep + got.astype(jnp.float32)
            low *= 2
    return blocks


def doubling_gather(x, axis):
    me = lax.axis_index(axis)
    step = 1
    while step < lax.axis_size(axis):
        other = lax.ppermute(x, axis, partner(axis, step))
        first = (me // step) % 2 == 0
        x = jnp.where(first, jnp.concatenate([x, other]), jnp.concatenate([other, x]))
        step *= 2
    return x


def patch_matrix(slab, planes, y_cells, x_cells):
    channels = slab.shape[2]
    cells = planes * y_cells * x_cells
    shifted = jnp.stack([slab[:, :, :, dx : dx + x_cells] for dx in range(3)])

    def body(src_ref, out_ref):
        dz = pl.program_id(0)
        for dy in range(3):
            for dx in range(3):
                row = (dy * 3 + dx) * channels
                for z in range(planes):
                    for y in range(y_cells):
                        out_ref[pl.ds(row, channels), pl.ds((z * y_cells + y) * x_cells, x_cells)] = (
                            src_ref[dx, z + dz, y + dy]
                        )

    return pl.pallas_call(
        body,
        grid=(3,),
        in_specs=[pl.BlockSpec(shifted.shape, lambda dz: (0, 0, 0, 0, 0))],
        out_specs=pl.BlockSpec((9 * channels, cells), lambda dz: (dz, 0)),
        out_shape=jax.ShapeDtypeStruct((27 * channels, cells), slab.dtype),
    )(shifted)


def tap_order(channels, n_taps):
    size = channels * n_taps
    new = jnp.arange(size, dtype=jnp.int32)
    old = (new % n_taps) * channels + new // n_taps
    return (old[:, None] == jnp.arange(size, dtype=jnp.int32)[None, :]).astype(jnp.bfloat16)


def halving_order(channels, n_taps, rows, axis):
    size = channels * n_taps
    bits = lax.axis_size(axis).bit_length() - 1
    spot = jnp.arange(size, dtype=jnp.int32)
    rank = spot // rows
    flipped = sum(((rank >> b) & 1) << (bits - 1 - b) for b in range(bits))
    block = jnp.bitwise_xor(flipped, lax.axis_index(axis))
    original = block * rows + spot % rows
    source = (original % n_taps) * channels + original // n_taps
    return (source[:, None] == jnp.arange(size, dtype=jnp.int32)[None, :]).astype(jnp.bfloat16)


def block_order(n_grains, n_taps, grain):
    size = n_grains * n_taps * grain
    old = jnp.arange(size, dtype=jnp.int32)
    new = ((old // (n_taps * grain)) * grain + old % grain) * n_taps + (old // grain) % n_taps
    return (jnp.arange(size, dtype=jnp.int32)[:, None] == new[None, :]).astype(jnp.float32)


def on_device(volume, out_grad, kernel, sample_idx, a_inverse, g_inverse):
    highest = lax.Precision.HIGHEST
    f32 = jnp.float32
    channels = volume.shape[1]
    planes = volume.shape[2]
    y_cells = volume.shape[3]
    x_cells = volume.shape[4]
    cells = planes * y_cells * x_cells
    patch = kernel.shape[1]
    n_taps = patch // channels
    n_dp = lax.axis_size("dp")
    n_sp = lax.axis_size("space")
    row_ch = channels // n_dp
    col_ch = channels // n_sp
    grain = math.gcd(row_ch, col_ch)
    n_grains = channels // grain
    contract_cells = (((1,), (1,)), ((), ()))

    block = padded_2(volume, (("space", 2),), 1)
    padded = jnp.pad(block[0], ((0, 0), (0, 0), (1, 1), (1, 1)))
    slab = jnp.transpose(padded, (1, 2, 0, 3))
    patches_t = patch_matrix(slab, planes, y_cells, x_cells)
    grad_flat = out_grad[0].reshape(channels, cells)
    kernel_perm = kernel.reshape(channels, channels, n_taps).transpose(0, 2, 1).reshape(channels, patch)

    grad_perm = lax.dot_general(grad_flat, patches_t, contract_cells, preferred_element_type=f32)
    g_part = lax.dot_general(grad_flat, grad_flat, contract_cells, preferred_element_type=f32)
    terms = jnp.concatenate([grad_perm, g_part], axis=1)
    terms, patches_t = lax.optimization_barrier((terms, patches_t))
    plane = butterfly_sum(terms, ("dp",))
    grad_plane = (
        plane[:, :patch].reshape(channels, n_taps, channels).transpose(0, 2, 1).reshape(channels, patch)
    )
    own_cols = halving_scatter(
        grad_plane.reshape(channels, n_sp, patch // n_sp), "space", 1, wire=f32
    ).reshape(channels, patch // n_sp)
    left = jnp.dot(g_inverse, own_cols, precision=highest)
    partial = jnp.dot(left, a_inverse, precision=highest)
    both = butterfly_sum(jnp.concatenate([partial, plane[:, patch:]], axis=1), ("space",))
    pre_grad = both[:, :patch]
    g_factor = both[:, patch:]


    cell_ids = sample_idx[0]
    counts = jnp.sum(
        (cell_ids[:, None] == jnp.arange(cells, dtype=jnp.int32)[None, :]).astype(f32), axis=0
    )
    weighted = (patches_t.astype(f32) * counts[None, :]).astype(jnp.bfloat16)
    total_samples = sample_idx.shape[1] * n_sp * n_dp
    a_perm = lax.dot_general(
        weighted, patches_t, contract_cells, preferred_element_type=f32
    ) / jnp.float32(total_samples)
    rows = patch // n_dp
    cols = patch // n_sp
    order, placed, a_bf = lax.optimization_barrier(
        (tap_order(channels, n_taps), halving_order(channels, n_taps, rows, "dp"), a_perm.astype(jnp.bfloat16))
    )
    a_rows = jnp.dot(placed, a_bf, preferred_element_type=f32)
    a_orig, kernel_perm = lax.optimization_barrier((a_rows, kernel_perm))
    forward = jnp.dot(kernel_perm, patches_t, preferred_element_type=f32)
    conv_out = forward.astype(jnp.bfloat16).reshape(1, channels, planes, y_cells, x_cells)
    step = 1
    while step < n_dp:
        half = a_orig.shape[0] // 2
        got = lax.ppermute(a_orig[half:].astype(jnp.bfloat16), "dp", partner("dp", step))
        a_orig = a_orig[:half] + got.astype(f32)
        step *= 2
    a_block = lax.dot_general(
        a_orig, order.astype(f32), contract_cells, precision=lax.Precision.HIGH
    )
    a_factor = quad_scatter(a_block.reshape(rows, n_sp, cols), "space", 1).reshape(rows, cols)
    return (conv_out, a_factor, g_factor, pre_grad)


def solution(mesh):
    placed = (
        P("dp", None, "space", None, None),
        P("dp", None, "space", None, None),
        P(),
        P("dp", "space"),
        P("space", None),
        P(),
    )
    return jax.shard_map(
        on_device,
        mesh=mesh,
        in_specs=placed,
        out_specs=(P("dp", None, "space", None, None), P("dp", "space"), P(), P()),
        check_vma=False,
    )
```

```python
import math

import jax
import jax.numpy as jnp
from jax import lax
from jax.experimental import pallas as pl
from jax.sharding import PartitionSpec as P


def padded_2(cells, sides, width):
    for axis, dim in sides:
        count = lax.axis_size(axis)
        ends = count - 1
        head = lax.slice_in_dim(cells, 0, width, axis=dim)
        tail = lax.slice_in_dim(cells, cells.shape[dim] - width, cells.shape[dim], axis=dim)
        cells = jnp.concatenate(
            [
                lax.ppermute(tail, axis, [(i, (i + 1) % count) for i in range(ends)]),
                cells,
                lax.ppermute(head, axis, [((i + 1) % count, i) for i in range(ends)]),
            ],
            axis=dim,
        )
    return cells


def partner(axis, step):
    return [(i, i ^ step) for i in range(lax.axis_size(axis))]


def butterfly_sum(x, axes):
    for axis in axes:
        size = lax.axis_size(axis)
        low = 1
        while low < size:
            high = low * 2
            got = lax.ppermute(x, axis, partner(axis, low))
            if high < size:
                pair = lax.ppermute(x, axis, partner(axis, high))
                other = lax.ppermute(x, axis, partner(axis, low + high))
                x = (x + got) + (pair + other)
                low = high * 2
            else:
                x = x + got
                low = high
    return x


def halving_scatter(blocks, axis, dim, wire=jnp.bfloat16):
    me = lax.axis_index(axis)
    step = 1
    while step < lax.axis_size(axis):
        shape = blocks.shape
        split = blocks.reshape(shape[:dim] + (shape[dim] // 2, 2) + shape[dim + 1 :])
        bit = (me // step) % 2
        keep = lax.dynamic_index_in_dim(split, bit, axis=dim + 1, keepdims=False)
        send = lax.dynamic_index_in_dim(split, 1 - bit, axis=dim + 1, keepdims=False)
        got = lax.ppermute(send.astype(wire), axis, partner(axis, step))
        blocks = keep + got.astype(jnp.float32)
        step *= 2
    return blocks


def quad_scatter(blocks, axis, dim, wire=jnp.bfloat16):
    me = lax.axis_index(axis)
    low = 1
    while low < lax.axis_size(axis):
        shape = blocks.shape
        if low * 2 < lax.axis_size(axis):
            split = blocks.reshape(shape[:dim] + (shape[dim] // 4, 4) + shape[dim + 1 :])
            digit = (me // low) % 4

            def pick(d):
                return lax.dynamic_index_in_dim(split, d, axis=dim + 1, keepdims=False)

            got = [
                lax.ppermute(pick(digit ^ k).astype(wire), axis, partner(axis, k * low)).astype(
                    jnp.float32
                )
                for k in (1, 2, 3)
            ]
            blocks = (pick(digit) + got[0]) + (got[1] + got[2])
            low *= 4
        else:
            split = blocks.reshape(shape[:dim] + (shape[dim] // 2, 2) + shape[dim + 1 :])
            bit = (me // low) % 2
            keep = lax.dynamic_index_in_dim(split, bit, axis=dim + 1, keepdims=False)
            send = lax.dynamic_index_in_dim(split, 1 - bit, axis=dim + 1, keepdims=False)
            got = lax.ppermute(send.astype(wire), axis, partner(axis, low))
            blocks = keep + got.astype(jnp.float32)
            low *= 2
    return blocks


def doubling_gather(x, axis):
    me = lax.axis_index(axis)
    step = 1
    while step < lax.axis_size(axis):
        other = lax.ppermute(x, axis, partner(axis, step))
        first = (me // step) % 2 == 0
        x = jnp.where(first, jnp.concatenate([x, other]), jnp.concatenate([other, x]))
        step *= 2
    return x


def patch_matrix(slab, planes, y_cells, x_cells):
    channels = slab.shape[2]
    cells = planes * y_cells * x_cells
    shifted = jnp.stack([slab[:, :, :, dx : dx + x_cells] for dx in range(3)])

    def body(src_ref, out_ref):
        dz = pl.program_id(0)
        for dy in range(3):
            for dx in range(3):
                row = (dy * 3 + dx) * channels
                for z in range(planes):
                    for y in range(y_cells):
                        out_ref[pl.ds(row, channels), pl.ds((z * y_cells + y) * x_cells, x_cells)] = (
                            src_ref[dx, z + dz, y + dy]
                        )

    return pl.pallas_call(
        body,
        grid=(3,),
        in_specs=[pl.BlockSpec(shifted.shape, lambda dz: (0, 0, 0, 0, 0))],
        out_specs=pl.BlockSpec((9 * channels, cells), lambda dz: (dz, 0)),
        out_shape=jax.ShapeDtypeStruct((27 * channels, cells), slab.dtype),
    )(shifted)


def tap_order(channels, n_taps):
    size = channels * n_taps
    new = jnp.arange(size, dtype=jnp.int32)
    old = (new % n_taps) * channels + new // n_taps
    return (old[:, None] == jnp.arange(size, dtype=jnp.int32)[None, :]).astype(jnp.bfloat16)


def halving_order(channels, n_taps, rows, axis):
    size = channels * n_taps
    bits = lax.axis_size(axis).bit_length() - 1
    spot = jnp.arange(size, dtype=jnp.int32)
    rank = spot // rows
    flipped = sum(((rank >> b) & 1) << (bits - 1 - b) for b in range(bits))
    block = jnp.bitwise_xor(flipped, lax.axis_index(axis))
    original = block * rows + spot % rows
    source = (original % n_taps) * channels + original // n_taps
    return (source[:, None] == jnp.arange(size, dtype=jnp.int32)[None, :]).astype(jnp.bfloat16)


def block_order(n_grains, n_taps, grain):
    size = n_grains * n_taps * grain
    old = jnp.arange(size, dtype=jnp.int32)
    new = ((old // (n_taps * grain)) * grain + old % grain) * n_taps + (old // grain) % n_taps
    return (jnp.arange(size, dtype=jnp.int32)[:, None] == new[None, :]).astype(jnp.float32)


def on_device(volume, out_grad, kernel, sample_idx, a_inverse, g_inverse):
    highest = lax.Precision.HIGHEST
    f32 = jnp.float32
    channels = volume.shape[1]
    planes = volume.shape[2]
    y_cells = volume.shape[3]
    x_cells = volume.shape[4]
    cells = planes * y_cells * x_cells
    patch = kernel.shape[1]
    n_taps = patch // channels
    n_dp = lax.axis_size("dp")
    n_sp = lax.axis_size("space")
    row_ch = channels // n_dp
    col_ch = channels // n_sp
    grain = math.gcd(row_ch, col_ch)
    n_grains = channels // grain
    contract_cells = (((1,), (1,)), ((), ()))

    block = padded_2(volume, (("space", 2),), 1)
    padded = jnp.pad(block[0], ((0, 0), (0, 0), (1, 1), (1, 1)))
    slab = jnp.transpose(padded, (1, 2, 0, 3))
    patches_t = patch_matrix(slab, planes, y_cells, x_cells)
    grad_flat = out_grad[0].reshape(channels, cells)
    kernel_perm = kernel.reshape(channels, channels, n_taps).transpose(0, 2, 1).reshape(channels, patch)

    grad_perm = lax.dot_general(grad_flat, patches_t, contract_cells, preferred_element_type=f32)
    g_part = lax.dot_general(grad_flat, grad_flat, contract_cells, preferred_element_type=f32)
    terms = jnp.concatenate([grad_perm, g_part], axis=1)
    terms, patches_t = lax.optimization_barrier((terms, patches_t))
    plane = butterfly_sum(terms, ("dp",))
    grad_plane = (
        plane[:, :patch].reshape(channels, n_taps, channels).transpose(0, 2, 1).reshape(channels, patch)
    )
    own_cols = quad_scatter(
        grad_plane.reshape(channels, n_sp, patch // n_sp), "space", 1, wire=f32
    ).reshape(channels, patch // n_sp)
    left = jnp.dot(g_inverse, own_cols, precision=highest)
    partial = jnp.dot(left, a_inverse, precision=highest)
    both = butterfly_sum(jnp.concatenate([partial, plane[:, patch:]], axis=1), ("space",))
    pre_grad = both[:, :patch]
    g_factor = both[:, patch:]


    cell_ids = sample_idx[0]
    counts = jnp.sum(
        (cell_ids[:, None] == jnp.arange(cells, dtype=jnp.int32)[None, :]).astype(f32), axis=0
    )
    weighted = (patches_t.astype(f32) * counts[None, :]).astype(jnp.bfloat16)
    total_samples = sample_idx.shape[1] * n_sp * n_dp
    a_perm = lax.dot_general(
        weighted, patches_t, contract_cells, preferred_element_type=f32
    ) / jnp.float32(total_samples)
    rows = patch // n_dp
    cols = patch // n_sp
    order, placed, a_bf = lax.optimization_barrier(
        (tap_order(channels, n_taps), halving_order(channels, n_taps, rows, "dp"), a_perm.astype(jnp.bfloat16))
    )
    a_rows = jnp.dot(placed, a_bf, preferred_element_type=f32)
    a_orig, kernel_perm = lax.optimization_barrier((a_rows, kernel_perm))
    forward = jnp.dot(kernel_perm, patches_t, preferred_element_type=f32)
    conv_out = forward.astype(jnp.bfloat16).reshape(1, channels, planes, y_cells, x_cells)
    step = 1
    while step < n_dp:
        half = a_orig.shape[0] // 2
        got = lax.ppermute(a_orig[half:].astype(jnp.bfloat16), "dp", partner("dp", step))
        a_orig = a_orig[:half] + got.astype(f32)
        step *= 2
    a_block = lax.dot_general(
        a_orig, order.astype(f32), contract_cells, precision=lax.Precision.HIGH
    )
    a_factor = quad_scatter(a_block.reshape(rows, n_sp, cols), "space", 1).reshape(rows, cols)
    return (conv_out, a_factor, g_factor, pre_grad)


def solution(mesh):
    placed = (
        P("dp", None, "space", None, None),
        P("dp", None, "space", None, None),
        P(),
        P("dp", "space"),
        P("space", None),
        P(),
    )
    return jax.shard_map(
        on_device,
        mesh=mesh,
        in_specs=placed,
        out_specs=(P("dp", None, "space", None, None), P("dp", "space"), P(), P()),
        check_vma=False,
    )
```

```python
import math

import jax
import jax.numpy as jnp
from jax import lax
from jax.experimental import pallas as pl
from jax.sharding import PartitionSpec as P


def padded_2(cells, sides, width):
    for axis, dim in sides:
        count = lax.axis_size(axis)
        ends = count - 1
        head = lax.slice_in_dim(cells, 0, width, axis=dim)
        tail = lax.slice_in_dim(cells, cells.shape[dim] - width, cells.shape[dim], axis=dim)
        cells = jnp.concatenate(
            [
                lax.ppermute(tail, axis, [(i, (i + 1) % count) for i in range(ends)]),
                cells,
                lax.ppermute(head, axis, [((i + 1) % count, i) for i in range(ends)]),
            ],
            axis=dim,
        )
    return cells


def partner(axis, step):
    return [(i, i ^ step) for i in range(lax.axis_size(axis))]


def butterfly_sum(x, axes):
    for axis in axes:
        size = lax.axis_size(axis)
        low = 1
        while low < size:
            high = low * 2
            got = lax.ppermute(x, axis, partner(axis, low))
            if high < size:
                pair = lax.ppermute(x, axis, partner(axis, high))
                other = lax.ppermute(x, axis, partner(axis, low + high))
                x = (x + got) + (pair + other)
                low = high * 2
            else:
                x = x + got
                low = high
    return x


def halving_scatter(blocks, axis, dim, wire=jnp.bfloat16):
    me = lax.axis_index(axis)
    step = 1
    while step < lax.axis_size(axis):
        shape = blocks.shape
        split = blocks.reshape(shape[:dim] + (shape[dim] // 2, 2) + shape[dim + 1 :])
        bit = (me // step) % 2
        keep = lax.dynamic_index_in_dim(split, bit, axis=dim + 1, keepdims=False)
        send = lax.dynamic_index_in_dim(split, 1 - bit, axis=dim + 1, keepdims=False)
        got = lax.ppermute(send.astype(wire), axis, partner(axis, step))
        blocks = keep + got.astype(jnp.float32)
        step *= 2
    return blocks


def quad_scatter(blocks, axis, dim, wire=jnp.bfloat16):
    me = lax.axis_index(axis)
    low = 1
    while low < lax.axis_size(axis):
        shape = blocks.shape
        if low * 2 < lax.axis_size(axis):
            split = blocks.reshape(shape[:dim] + (shape[dim] // 4, 4) + shape[dim + 1 :])
            digit = (me // low) % 4

            def pick(d):
                return lax.dynamic_index_in_dim(split, d, axis=dim + 1, keepdims=False)

            got = [
                lax.ppermute(pick(digit ^ k).astype(wire), axis, partner(axis, k * low)).astype(
                    jnp.float32
                )
                for k in (1, 2, 3)
            ]
            blocks = (pick(digit) + got[0]) + (got[1] + got[2])
            low *= 4
        else:
            split = blocks.reshape(shape[:dim] + (shape[dim] // 2, 2) + shape[dim + 1 :])
            bit = (me // low) % 2
            keep = lax.dynamic_index_in_dim(split, bit, axis=dim + 1, keepdims=False)
            send = lax.dynamic_index_in_dim(split, 1 - bit, axis=dim + 1, keepdims=False)
            got = lax.ppermute(send.astype(wire), axis, partner(axis, low))
            blocks = keep + got.astype(jnp.float32)
            low *= 2
    return blocks


def doubling_gather(x, axis):
    me = lax.axis_index(axis)
    step = 1
    while step < lax.axis_size(axis):
        other = lax.ppermute(x, axis, partner(axis, step))
        first = (me // step) % 2 == 0
        x = jnp.where(first, jnp.concatenate([x, other]), jnp.concatenate([other, x]))
        step *= 2
    return x


def patch_matrix(slab, planes, y_cells, x_cells):
    channels = slab.shape[2]
    cells = planes * y_cells * x_cells
    shifted = jnp.stack([slab[:, :, :, dx : dx + x_cells] for dx in range(3)])

    def body(src_ref, out_ref):
        dz = pl.program_id(0)
        for dy in range(3):
            for dx in range(3):
                row = (dy * 3 + dx) * channels
                for z in range(planes):
                    for y in range(y_cells):
                        out_ref[pl.ds(row, channels), pl.ds((z * y_cells + y) * x_cells, x_cells)] = (
                            src_ref[dx, z + dz, y + dy]
                        )

    return pl.pallas_call(
        body,
        grid=(3,),
        in_specs=[pl.BlockSpec(shifted.shape, lambda dz: (0, 0, 0, 0, 0))],
        out_specs=pl.BlockSpec((9 * channels, cells), lambda dz: (dz, 0)),
        out_shape=jax.ShapeDtypeStruct((27 * channels, cells), slab.dtype),
    )(shifted)


def tap_order(channels, n_taps):
    size = channels * n_taps
    new = jnp.arange(size, dtype=jnp.int32)
    old = (new % n_taps) * channels + new // n_taps
    return (old[:, None] == jnp.arange(size, dtype=jnp.int32)[None, :]).astype(jnp.bfloat16)


def halving_order(channels, n_taps, rows, axis):
    size = channels * n_taps
    bits = lax.axis_size(axis).bit_length() - 1
    spot = jnp.arange(size, dtype=jnp.int32)
    rank = spot // rows
    flipped = sum(((rank >> b) & 1) << (bits - 1 - b) for b in range(bits))
    block = jnp.bitwise_xor(flipped, lax.axis_index(axis))
    original = block * rows + spot % rows
    source = (original % n_taps) * channels + original // n_taps
    return (source[:, None] == jnp.arange(size, dtype=jnp.int32)[None, :]).astype(jnp.bfloat16)


def block_order(n_grains, n_taps, grain):
    size = n_grains * n_taps * grain
    old = jnp.arange(size, dtype=jnp.int32)
    new = ((old // (n_taps * grain)) * grain + old % grain) * n_taps + (old // grain) % n_taps
    return (jnp.arange(size, dtype=jnp.int32)[:, None] == new[None, :]).astype(jnp.float32)


def on_device(volume, out_grad, kernel, sample_idx, a_inverse, g_inverse):
    highest = lax.Precision.HIGHEST
    f32 = jnp.float32
    channels = volume.shape[1]
    planes = volume.shape[2]
    y_cells = volume.shape[3]
    x_cells = volume.shape[4]
    cells = planes * y_cells * x_cells
    patch = kernel.shape[1]
    n_taps = patch // channels
    n_dp = lax.axis_size("dp")
    n_sp = lax.axis_size("space")
    row_ch = channels // n_dp
    col_ch = channels // n_sp
    grain = math.gcd(row_ch, col_ch)
    n_grains = channels // grain
    contract_cells = (((1,), (1,)), ((), ()))

    block = padded_2(volume, (("space", 2),), 1)
    padded = jnp.pad(block[0], ((0, 0), (0, 0), (1, 1), (1, 1)))
    slab = jnp.transpose(padded, (1, 2, 0, 3))
    patches_t = patch_matrix(slab, planes, y_cells, x_cells)
    grad_flat = out_grad[0].reshape(channels, cells)
    kernel_perm = kernel.reshape(channels, channels, n_taps).transpose(0, 2, 1).reshape(channels, patch)

    grad_perm = lax.dot_general(grad_flat, patches_t, contract_cells, preferred_element_type=f32)
    g_part = lax.dot_general(grad_flat, grad_flat, contract_cells, preferred_element_type=f32)
    terms = jnp.concatenate([grad_perm, g_part], axis=1)
    terms, patches_t = lax.optimization_barrier((terms, patches_t))
    plane = butterfly_sum(terms, ("dp",))
    grad_plane = (
        plane[:, :patch].reshape(channels, n_taps, channels).transpose(0, 2, 1).reshape(channels, patch)
    )
    own_cols = quad_scatter(
        grad_plane.reshape(channels, n_sp, patch // n_sp), "space", 1, wire=f32
    ).reshape(channels, patch // n_sp)
    left = jnp.dot(g_inverse, own_cols, precision=highest)
    partial = jnp.dot(left, a_inverse, precision=highest)
    both = butterfly_sum(jnp.concatenate([partial, plane[:, patch:]], axis=1), ("space",))
    pre_grad = both[:, :patch]
    g_factor = both[:, patch:]


    cell_ids = sample_idx[0]
    counts = jnp.sum(
        (cell_ids[:, None] == jnp.arange(cells, dtype=jnp.int32)[None, :]).astype(f32), axis=0
    )
    weighted = (patches_t.astype(f32) * counts[None, :]).astype(jnp.bfloat16)
    total_samples = sample_idx.shape[1] * n_sp * n_dp
    a_perm = lax.dot_general(
        weighted, patches_t, contract_cells, preferred_element_type=f32
    ) / jnp.float32(total_samples)
    rows = patch // n_dp
    cols = patch // n_sp
    order, placed, a_bf = lax.optimization_barrier(
        (tap_order(channels, n_taps), halving_order(channels, n_taps, rows, "dp"), a_perm.astype(jnp.bfloat16))
    )
    a_rows = jnp.dot(placed, a_bf, preferred_element_type=f32)
    a_orig, kernel_perm = lax.optimization_barrier((a_rows, kernel_perm))
    forward = jnp.dot(kernel_perm, patches_t, preferred_element_type=f32)
    conv_out = forward.astype(jnp.bfloat16).reshape(1, channels, planes, y_cells, x_cells)
    step = 1
    if n_dp >= 4:
        quarter = a_orig.shape[0] // 4
        got = [
            lax.ppermute(
                a_orig[((s & 1) * 2 + (s >> 1)) * quarter :][:quarter].astype(jnp.bfloat16),
                "dp",
                partner("dp", s),
            ).astype(f32)
            for s in (1, 2, 3)
        ]
        a_orig = (a_orig[:quarter] + got[0]) + (got[1] + got[2])
        step = 4
    while step < n_dp:
        half = a_orig.shape[0] // 2
        got = lax.ppermute(a_orig[half:].astype(jnp.bfloat16), "dp", partner("dp", step))
        a_orig = a_orig[:half] + got.astype(f32)
        step *= 2
    a_block = lax.dot_general(
        a_orig, order.astype(f32), contract_cells, precision=lax.Precision.HIGH
    )
    a_factor = quad_scatter(a_block.reshape(rows, n_sp, cols), "space", 1).reshape(rows, cols)
    return (conv_out, a_factor, g_factor, pre_grad)


def solution(mesh):
    placed = (
        P("dp", None, "space", None, None),
        P("dp", None, "space", None, None),
        P(),
        P("dp", "space"),
        P("space", None),
        P(),
    )
    return jax.shard_map(
        on_device,
        mesh=mesh,
        in_specs=placed,
        out_specs=(P("dp", None, "space", None, None), P("dp", "space"), P(), P()),
        check_vma=False,
    )
```

```python
import math

import jax
import jax.numpy as jnp
from jax import lax
from jax.experimental import pallas as pl
from jax.sharding import PartitionSpec as P


def padded_2(cells, sides, width):
    for axis, dim in sides:
        count = lax.axis_size(axis)
        ends = count - 1
        head = lax.slice_in_dim(cells, 0, width, axis=dim)
        tail = lax.slice_in_dim(cells, cells.shape[dim] - width, cells.shape[dim], axis=dim)
        cells = jnp.concatenate(
            [
                lax.ppermute(tail, axis, [(i, (i + 1) % count) for i in range(ends)]),
                cells,
                lax.ppermute(head, axis, [((i + 1) % count, i) for i in range(ends)]),
            ],
            axis=dim,
        )
    return cells


def partner(axis, step):
    return [(i, i ^ step) for i in range(lax.axis_size(axis))]


def butterfly_sum(x, axes):
    for axis in axes:
        size = lax.axis_size(axis)
        low = 1
        while low < size:
            high = low * 2
            got = lax.ppermute(x, axis, partner(axis, low))
            if high < size:
                pair = lax.ppermute(x, axis, partner(axis, high))
                other = lax.ppermute(x, axis, partner(axis, low + high))
                x = (x + got) + (pair + other)
                low = high * 2
            else:
                x = x + got
                low = high
    return x


def halving_scatter(blocks, axis, dim, wire=jnp.bfloat16):
    me = lax.axis_index(axis)
    step = 1
    while step < lax.axis_size(axis):
        shape = blocks.shape
        split = blocks.reshape(shape[:dim] + (shape[dim] // 2, 2) + shape[dim + 1 :])
        bit = (me // step) % 2
        keep = lax.dynamic_index_in_dim(split, bit, axis=dim + 1, keepdims=False)
        send = lax.dynamic_index_in_dim(split, 1 - bit, axis=dim + 1, keepdims=False)
        got = lax.ppermute(send.astype(wire), axis, partner(axis, step))
        blocks = keep + got.astype(jnp.float32)
        step *= 2
    return blocks


def quad_scatter(blocks, axis, dim, wire=jnp.bfloat16):
    me = lax.axis_index(axis)
    low = 1
    while low < lax.axis_size(axis):
        shape = blocks.shape
        if low * 2 < lax.axis_size(axis):
            split = blocks.reshape(shape[:dim] + (shape[dim] // 4, 4) + shape[dim + 1 :])
            digit = (me // low) % 4

            def pick(d):
                return lax.dynamic_index_in_dim(split, d, axis=dim + 1, keepdims=False)

            got = [
                lax.ppermute(pick(digit ^ k).astype(wire), axis, partner(axis, k * low)).astype(
                    jnp.float32
                )
                for k in (1, 2, 3)
            ]
            blocks = (pick(digit) + got[0]) + (got[1] + got[2])
            low *= 4
        else:
            split = blocks.reshape(shape[:dim] + (shape[dim] // 2, 2) + shape[dim + 1 :])
            bit = (me // low) % 2
            keep = lax.dynamic_index_in_dim(split, bit, axis=dim + 1, keepdims=False)
            send = lax.dynamic_index_in_dim(split, 1 - bit, axis=dim + 1, keepdims=False)
            got = lax.ppermute(send.astype(wire), axis, partner(axis, low))
            blocks = keep + got.astype(jnp.float32)
            low *= 2
    return blocks


def doubling_gather(x, axis):
    me = lax.axis_index(axis)
    step = 1
    while step < lax.axis_size(axis):
        other = lax.ppermute(x, axis, partner(axis, step))
        first = (me // step) % 2 == 0
        x = jnp.where(first, jnp.concatenate([x, other]), jnp.concatenate([other, x]))
        step *= 2
    return x


def patch_matrix(slab, planes, y_cells, x_cells):
    channels = slab.shape[2]
    cells = planes * y_cells * x_cells
    shifted = jnp.stack([slab[:, :, :, dx : dx + x_cells] for dx in range(3)])

    def body(src_ref, out_ref):
        dz = pl.program_id(0)
        for dy in range(3):
            for dx in range(3):
                row = (dy * 3 + dx) * channels
                for z in range(planes):
                    for y in range(y_cells):
                        out_ref[pl.ds(row, channels), pl.ds((z * y_cells + y) * x_cells, x_cells)] = (
                            src_ref[dx, z + dz, y + dy]
                        )

    return pl.pallas_call(
        body,
        grid=(3,),
        in_specs=[pl.BlockSpec(shifted.shape, lambda dz: (0, 0, 0, 0, 0))],
        out_specs=pl.BlockSpec((9 * channels, cells), lambda dz: (dz, 0)),
        out_shape=jax.ShapeDtypeStruct((27 * channels, cells), slab.dtype),
    )(shifted)


def tap_order(channels, n_taps):
    size = channels * n_taps
    new = jnp.arange(size, dtype=jnp.int32)
    old = (new % n_taps) * channels + new // n_taps
    return (old[:, None] == jnp.arange(size, dtype=jnp.int32)[None, :]).astype(jnp.bfloat16)


def halving_order(channels, n_taps, rows, axis):
    size = channels * n_taps
    bits = lax.axis_size(axis).bit_length() - 1
    spot = jnp.arange(size, dtype=jnp.int32)
    rank = spot // rows
    flipped = sum(((rank >> b) & 1) << (bits - 1 - b) for b in range(bits))
    block = jnp.bitwise_xor(flipped, lax.axis_index(axis))
    original = block * rows + spot % rows
    source = (original % n_taps) * channels + original // n_taps
    return (source[:, None] == jnp.arange(size, dtype=jnp.int32)[None, :]).astype(jnp.bfloat16)


def block_order(n_grains, n_taps, grain):
    size = n_grains * n_taps * grain
    old = jnp.arange(size, dtype=jnp.int32)
    new = ((old // (n_taps * grain)) * grain + old % grain) * n_taps + (old // grain) % n_taps
    return (jnp.arange(size, dtype=jnp.int32)[:, None] == new[None, :]).astype(jnp.float32)


def on_device(volume, out_grad, kernel, sample_idx, a_inverse, g_inverse):
    highest = lax.Precision.HIGHEST
    f32 = jnp.float32
    channels = volume.shape[1]
    planes = volume.shape[2]
    y_cells = volume.shape[3]
    x_cells = volume.shape[4]
    cells = planes * y_cells * x_cells
    patch = kernel.shape[1]
    n_taps = patch // channels
    n_dp = lax.axis_size("dp")
    n_sp = lax.axis_size("space")
    row_ch = channels // n_dp
    col_ch = channels // n_sp
    grain = math.gcd(row_ch, col_ch)
    n_grains = channels // grain
    contract_cells = (((1,), (1,)), ((), ()))

    block = padded_2(volume, (("space", 2),), 1)
    padded = jnp.pad(block[0], ((0, 0), (0, 0), (1, 1), (1, 1)))
    slab = jnp.transpose(padded, (1, 2, 0, 3))
    patches_t = patch_matrix(slab, planes, y_cells, x_cells)
    grad_flat = out_grad[0].reshape(channels, cells)
    kernel_perm = kernel.reshape(channels, channels, n_taps).transpose(0, 2, 1).reshape(channels, patch)

    grad_perm = lax.dot_general(grad_flat, patches_t, contract_cells, preferred_element_type=f32)
    g_part = lax.dot_general(grad_flat, grad_flat, contract_cells, preferred_element_type=f32)
    terms = jnp.concatenate([grad_perm, g_part], axis=1)
    terms, patches_t = lax.optimization_barrier((terms, patches_t))
    plane = butterfly_sum(terms, ("dp",))
    grad_plane = (
        plane[:, :patch].reshape(channels, n_taps, channels).transpose(0, 2, 1).reshape(channels, patch)
    )
    own_cols = quad_scatter(
        grad_plane.reshape(channels, n_sp, patch // n_sp), "space", 1, wire=f32
    ).reshape(channels, patch // n_sp)
    left = jnp.dot(g_inverse, own_cols, precision=highest)
    partial = jnp.dot(left, a_inverse, precision=highest)
    both = butterfly_sum(jnp.concatenate([partial, plane[:, patch:]], axis=1), ("space",))
    pre_grad = both[:, :patch]
    g_factor = both[:, patch:]


    cell_ids = sample_idx[0]
    counts = jnp.sum(
        (cell_ids[:, None] == jnp.arange(cells, dtype=jnp.int32)[None, :]).astype(f32), axis=0
    )
    weighted = (patches_t.astype(f32) * counts[None, :]).astype(jnp.bfloat16)
    total_samples = sample_idx.shape[1] * n_sp * n_dp
    a_perm = lax.dot_general(
        weighted, patches_t, contract_cells, preferred_element_type=f32
    ) / jnp.float32(total_samples)
    rows = patch // n_dp
    cols = patch // n_sp
    order, placed, a_bf = lax.optimization_barrier(
        (tap_order(channels, n_taps), halving_order(channels, n_taps, rows, "dp"), a_perm.astype(jnp.bfloat16))
    )
    a_rows = jnp.dot(placed, a_bf, preferred_element_type=f32)
    a_orig, kernel_perm = lax.optimization_barrier((a_rows, kernel_perm))
    forward = jnp.dot(kernel_perm, patches_t, preferred_element_type=f32)
    conv_out = forward.astype(jnp.bfloat16).reshape(1, channels, planes, y_cells, x_cells)
    step = 1
    if n_dp >= 2:
        quarter = a_orig.shape[0] // 4
        got = [
            lax.ppermute(a_orig[(2 + q) * quarter :][:quarter].astype(jnp.bfloat16), "dp", partner("dp", 1))
            for q in (0, 1)
        ]
        a_orig = jnp.concatenate(
            [a_orig[q * quarter :][:quarter] + got[q].astype(f32) for q in (0, 1)], axis=0
        )
        step = 2
    while step < n_dp:
        half = a_orig.shape[0] // 2
        got = lax.ppermute(a_orig[half:].astype(jnp.bfloat16), "dp", partner("dp", step))
        a_orig = a_orig[:half] + got.astype(f32)
        step *= 2
    a_block = lax.dot_general(
        a_orig, order.astype(f32), contract_cells, precision=lax.Precision.HIGH
    )
    a_factor = quad_scatter(a_block.reshape(rows, n_sp, cols), "space", 1).reshape(rows, cols)
    return (conv_out, a_factor, g_factor, pre_grad)


def solution(mesh):
    placed = (
        P("dp", None, "space", None, None),
        P("dp", None, "space", None, None),
        P(),
        P("dp", "space"),
        P("space", None),
        P(),
    )
    return jax.shard_map(
        on_device,
        mesh=mesh,
        in_specs=placed,
        out_specs=(P("dp", None, "space", None, None), P("dp", "space"), P(), P()),
        check_vma=False,
    )
```

```python
import math

import jax
import jax.numpy as jnp
from jax import lax
from jax.experimental import pallas as pl
from jax.sharding import PartitionSpec as P


def padded_2(cells, sides, width):
    for axis, dim in sides:
        count = lax.axis_size(axis)
        ends = count - 1
        head = lax.slice_in_dim(cells, 0, width, axis=dim)
        tail = lax.slice_in_dim(cells, cells.shape[dim] - width, cells.shape[dim], axis=dim)
        cells = jnp.concatenate(
            [
                lax.ppermute(tail, axis, [(i, (i + 1) % count) for i in range(ends)]),
                cells,
                lax.ppermute(head, axis, [((i + 1) % count, i) for i in range(ends)]),
            ],
            axis=dim,
        )
    return cells


def partner(axis, step):
    return [(i, i ^ step) for i in range(lax.axis_size(axis))]


def butterfly_sum(x, axes):
    for axis in axes:
        size = lax.axis_size(axis)
        low = 1
        while low < size:
            high = low * 2
            got = lax.ppermute(x, axis, partner(axis, low))
            if high < size:
                pair = lax.ppermute(x, axis, partner(axis, high))
                other = lax.ppermute(x, axis, partner(axis, low + high))
                x = (x + got) + (pair + other)
                low = high * 2
            else:
                x = x + got
                low = high
    return x


def halving_scatter(blocks, axis, dim, wire=jnp.bfloat16):
    me = lax.axis_index(axis)
    step = 1
    while step < lax.axis_size(axis):
        shape = blocks.shape
        split = blocks.reshape(shape[:dim] + (shape[dim] // 2, 2) + shape[dim + 1 :])
        bit = (me // step) % 2
        keep = lax.dynamic_index_in_dim(split, bit, axis=dim + 1, keepdims=False)
        send = lax.dynamic_index_in_dim(split, 1 - bit, axis=dim + 1, keepdims=False)
        got = lax.ppermute(send.astype(wire), axis, partner(axis, step))
        blocks = keep + got.astype(jnp.float32)
        step *= 2
    return blocks


def quad_scatter(blocks, axis, dim, wire=jnp.bfloat16):
    me = lax.axis_index(axis)
    low = 1
    while low < lax.axis_size(axis):
        shape = blocks.shape
        if low * 2 < lax.axis_size(axis):
            split = blocks.reshape(shape[:dim] + (shape[dim] // 4, 4) + shape[dim + 1 :])
            digit = (me // low) % 4

            def pick(d):
                return lax.dynamic_index_in_dim(split, d, axis=dim + 1, keepdims=False)

            got = [
                lax.ppermute(pick(digit ^ k).astype(wire), axis, partner(axis, k * low)).astype(
                    jnp.float32
                )
                for k in (1, 2, 3)
            ]
            blocks = (pick(digit) + got[0]) + (got[1] + got[2])
            low *= 4
        else:
            split = blocks.reshape(shape[:dim] + (shape[dim] // 2, 2) + shape[dim + 1 :])
            bit = (me // low) % 2
            keep = lax.dynamic_index_in_dim(split, bit, axis=dim + 1, keepdims=False)
            send = lax.dynamic_index_in_dim(split, 1 - bit, axis=dim + 1, keepdims=False)
            got = lax.ppermute(send.astype(wire), axis, partner(axis, low))
            blocks = keep + got.astype(jnp.float32)
            low *= 2
    return blocks


def doubling_gather(x, axis):
    me = lax.axis_index(axis)
    step = 1
    while step < lax.axis_size(axis):
        other = lax.ppermute(x, axis, partner(axis, step))
        first = (me // step) % 2 == 0
        x = jnp.where(first, jnp.concatenate([x, other]), jnp.concatenate([other, x]))
        step *= 2
    return x


def patch_matrix(slab, planes, y_cells, x_cells):
    channels = slab.shape[2]
    cells = planes * y_cells * x_cells
    shifted = jnp.stack([slab[:, :, :, dx : dx + x_cells] for dx in range(3)])

    def body(src_ref, out_ref):
        dz = pl.program_id(0)
        for dy in range(3):
            for dx in range(3):
                row = (dy * 3 + dx) * channels
                for z in range(planes):
                    for y in range(y_cells):
                        out_ref[pl.ds(row, channels), pl.ds((z * y_cells + y) * x_cells, x_cells)] = (
                            src_ref[dx, z + dz, y + dy]
                        )

    return pl.pallas_call(
        body,
        grid=(3,),
        in_specs=[pl.BlockSpec(shifted.shape, lambda dz: (0, 0, 0, 0, 0))],
        out_specs=pl.BlockSpec((9 * channels, cells), lambda dz: (dz, 0)),
        out_shape=jax.ShapeDtypeStruct((27 * channels, cells), slab.dtype),
    )(shifted)


def tap_order(channels, n_taps):
    size = channels * n_taps
    new = jnp.arange(size, dtype=jnp.int32)
    old = (new % n_taps) * channels + new // n_taps
    return (old[:, None] == jnp.arange(size, dtype=jnp.int32)[None, :]).astype(jnp.bfloat16)


def halving_order(channels, n_taps, rows, axis):
    size = channels * n_taps
    bits = lax.axis_size(axis).bit_length() - 1
    spot = jnp.arange(size, dtype=jnp.int32)
    rank = spot // rows
    flipped = sum(((rank >> b) & 1) << (bits - 1 - b) for b in range(bits))
    block = jnp.bitwise_xor(flipped, lax.axis_index(axis))
    original = block * rows + spot % rows
    source = (original % n_taps) * channels + original // n_taps
    return (source[:, None] == jnp.arange(size, dtype=jnp.int32)[None, :]).astype(jnp.bfloat16)


def block_order(n_grains, n_taps, grain):
    size = n_grains * n_taps * grain
    old = jnp.arange(size, dtype=jnp.int32)
    new = ((old // (n_taps * grain)) * grain + old % grain) * n_taps + (old // grain) % n_taps
    return (jnp.arange(size, dtype=jnp.int32)[:, None] == new[None, :]).astype(jnp.float32)


def on_device(volume, out_grad, kernel, sample_idx, a_inverse, g_inverse):
    highest = lax.Precision.HIGHEST
    f32 = jnp.float32
    channels = volume.shape[1]
    planes = volume.shape[2]
    y_cells = volume.shape[3]
    x_cells = volume.shape[4]
    cells = planes * y_cells * x_cells
    patch = kernel.shape[1]
    n_taps = patch // channels
    n_dp = lax.axis_size("dp")
    n_sp = lax.axis_size("space")
    row_ch = channels // n_dp
    col_ch = channels // n_sp
    grain = math.gcd(row_ch, col_ch)
    n_grains = channels // grain
    contract_cells = (((1,), (1,)), ((), ()))

    cell_ids = sample_idx[0]
    counts = jnp.sum(
        (cell_ids[:, None] == jnp.arange(cells, dtype=jnp.int32)[None, :]).astype(f32), axis=0
    )
    grad_flat = out_grad[0].reshape(channels, cells)
    g_part = lax.dot_general(grad_flat, grad_flat, contract_cells, preferred_element_type=f32)
    volume, counts, g_part = lax.optimization_barrier((volume, counts, g_part))
    block = padded_2(volume, (("space", 2),), 1)
    padded = jnp.pad(block[0], ((0, 0), (0, 0), (1, 1), (1, 1)))
    slab = jnp.transpose(padded, (1, 2, 0, 3))
    patches_t = patch_matrix(slab, planes, y_cells, x_cells)
    grad_flat = out_grad[0].reshape(channels, cells)
    kernel_perm = kernel.reshape(channels, channels, n_taps).transpose(0, 2, 1).reshape(channels, patch)

    grad_perm = lax.dot_general(grad_flat, patches_t, contract_cells, preferred_element_type=f32)
    terms = jnp.concatenate([grad_perm, g_part], axis=1)
    terms, patches_t = lax.optimization_barrier((terms, patches_t))
    plane = butterfly_sum(terms, ("dp",))
    grad_plane = (
        plane[:, :patch].reshape(channels, n_taps, channels).transpose(0, 2, 1).reshape(channels, patch)
    )
    own_cols = quad_scatter(
        grad_plane.reshape(channels, n_sp, patch // n_sp), "space", 1, wire=f32
    ).reshape(channels, patch // n_sp)
    left = jnp.dot(g_inverse, own_cols, precision=highest)
    partial = jnp.dot(left, a_inverse, precision=highest)
    both = butterfly_sum(jnp.concatenate([partial, plane[:, patch:]], axis=1), ("space",))
    pre_grad = both[:, :patch]
    g_factor = both[:, patch:]


    weighted = (patches_t.astype(f32) * counts[None, :]).astype(jnp.bfloat16)
    total_samples = sample_idx.shape[1] * n_sp * n_dp
    a_perm = lax.dot_general(
        weighted, patches_t, contract_cells, preferred_element_type=f32
    ) / jnp.float32(total_samples)
    rows = patch // n_dp
    cols = patch // n_sp
    order, placed, a_bf = lax.optimization_barrier(
        (tap_order(channels, n_taps), halving_order(channels, n_taps, rows, "dp"), a_perm.astype(jnp.bfloat16))
    )
    a_rows = jnp.dot(placed, a_bf, preferred_element_type=f32)
    a_orig, kernel_perm = lax.optimization_barrier((a_rows, kernel_perm))
    forward = jnp.dot(kernel_perm, patches_t, preferred_element_type=f32)
    conv_out = forward.astype(jnp.bfloat16).reshape(1, channels, planes, y_cells, x_cells)
    step = 1
    while step < n_dp:
        half = a_orig.shape[0] // 2
        got = lax.ppermute(a_orig[half:].astype(jnp.bfloat16), "dp", partner("dp", step))
        a_orig = a_orig[:half] + got.astype(f32)
        step *= 2
    a_block = lax.dot_general(
        a_orig, order.astype(f32), contract_cells, precision=lax.Precision.HIGH
    )
    a_factor = quad_scatter(a_block.reshape(rows, n_sp, cols), "space", 1).reshape(rows, cols)
    return (conv_out, a_factor, g_factor, pre_grad)


def solution(mesh):
    placed = (
        P("dp", None, "space", None, None),
        P("dp", None, "space", None, None),
        P(),
        P("dp", "space"),
        P("space", None),
        P(),
    )
    return jax.shard_map(
        on_device,
        mesh=mesh,
        in_specs=placed,
        out_specs=(P("dp", None, "space", None, None), P("dp", "space"), P(), P()),
        check_vma=False,
    )
```

```python
import math

import jax
import jax.numpy as jnp
from jax import lax
from jax.experimental import pallas as pl
from jax.sharding import PartitionSpec as P


def padded_2(cells, sides, width):
    for axis, dim in sides:
        count = lax.axis_size(axis)
        ends = count - 1
        head = lax.slice_in_dim(cells, 0, width, axis=dim)
        tail = lax.slice_in_dim(cells, cells.shape[dim] - width, cells.shape[dim], axis=dim)
        cells = jnp.concatenate(
            [
                lax.ppermute(tail, axis, [(i, (i + 1) % count) for i in range(ends)]),
                cells,
                lax.ppermute(head, axis, [((i + 1) % count, i) for i in range(ends)]),
            ],
            axis=dim,
        )
    return cells


def partner(axis, step):
    return [(i, i ^ step) for i in range(lax.axis_size(axis))]


def butterfly_sum(x, axes):
    for axis in axes:
        size = lax.axis_size(axis)
        low = 1
        while low < size:
            high = low * 2
            got = lax.ppermute(x, axis, partner(axis, low))
            if high < size:
                pair = lax.ppermute(x, axis, partner(axis, high))
                other = lax.ppermute(x, axis, partner(axis, low + high))
                x = (x + got) + (pair + other)
                low = high * 2
            else:
                x = x + got
                low = high
    return x


def halving_scatter(blocks, axis, dim, wire=jnp.bfloat16):
    me = lax.axis_index(axis)
    step = 1
    while step < lax.axis_size(axis):
        shape = blocks.shape
        split = blocks.reshape(shape[:dim] + (shape[dim] // 2, 2) + shape[dim + 1 :])
        bit = (me // step) % 2
        keep = lax.dynamic_index_in_dim(split, bit, axis=dim + 1, keepdims=False)
        send = lax.dynamic_index_in_dim(split, 1 - bit, axis=dim + 1, keepdims=False)
        got = lax.ppermute(send.astype(wire), axis, partner(axis, step))
        blocks = keep + got.astype(jnp.float32)
        step *= 2
    return blocks


def quad_scatter(blocks, axis, dim, wire=jnp.bfloat16):
    me = lax.axis_index(axis)
    low = 1
    while low < lax.axis_size(axis):
        shape = blocks.shape
        if low * 2 < lax.axis_size(axis):
            split = blocks.reshape(shape[:dim] + (shape[dim] // 4, 4) + shape[dim + 1 :])
            digit = (me // low) % 4

            def pick(d):
                return lax.dynamic_index_in_dim(split, d, axis=dim + 1, keepdims=False)

            got = [
                lax.ppermute(pick(digit ^ k).astype(wire), axis, partner(axis, k * low)).astype(
                    jnp.float32
                )
                for k in (1, 2, 3)
            ]
            blocks = (pick(digit) + got[0]) + (got[1] + got[2])
            low *= 4
        else:
            split = blocks.reshape(shape[:dim] + (shape[dim] // 2, 2) + shape[dim + 1 :])
            bit = (me // low) % 2
            keep = lax.dynamic_index_in_dim(split, bit, axis=dim + 1, keepdims=False)
            send = lax.dynamic_index_in_dim(split, 1 - bit, axis=dim + 1, keepdims=False)
            got = lax.ppermute(send.astype(wire), axis, partner(axis, low))
            blocks = keep + got.astype(jnp.float32)
            low *= 2
    return blocks


def doubling_gather(x, axis):
    me = lax.axis_index(axis)
    step = 1
    while step < lax.axis_size(axis):
        other = lax.ppermute(x, axis, partner(axis, step))
        first = (me // step) % 2 == 0
        x = jnp.where(first, jnp.concatenate([x, other]), jnp.concatenate([other, x]))
        step *= 2
    return x


def patch_matrix(slab, planes, y_cells, x_cells):
    channels = slab.shape[2]
    cells = planes * y_cells * x_cells
    shifted = jnp.stack([slab[:, :, :, dx : dx + x_cells] for dx in range(3)])

    def body(src_ref, out_ref):
        dz = pl.program_id(0)
        for dy in range(3):
            for dx in range(3):
                row = (dy * 3 + dx) * channels
                for z in range(planes):
                    for y in range(y_cells):
                        out_ref[pl.ds(row, channels), pl.ds((z * y_cells + y) * x_cells, x_cells)] = (
                            src_ref[dx, z + dz, y + dy]
                        )

    return pl.pallas_call(
        body,
        grid=(3,),
        in_specs=[pl.BlockSpec(shifted.shape, lambda dz: (0, 0, 0, 0, 0))],
        out_specs=pl.BlockSpec((9 * channels, cells), lambda dz: (dz, 0)),
        out_shape=jax.ShapeDtypeStruct((27 * channels, cells), slab.dtype),
    )(shifted)


def tap_order(channels, n_taps):
    size = channels * n_taps
    new = jnp.arange(size, dtype=jnp.int32)
    old = (new % n_taps) * channels + new // n_taps
    return (old[:, None] == jnp.arange(size, dtype=jnp.int32)[None, :]).astype(jnp.bfloat16)


def halving_order(channels, n_taps, rows, axis):
    size = channels * n_taps
    bits = lax.axis_size(axis).bit_length() - 1
    spot = jnp.arange(size, dtype=jnp.int32)
    rank = spot // rows
    flipped = sum(((rank >> b) & 1) << (bits - 1 - b) for b in range(bits))
    block = jnp.bitwise_xor(flipped, lax.axis_index(axis))
    original = block * rows + spot % rows
    source = (original % n_taps) * channels + original // n_taps
    return (source[:, None] == jnp.arange(size, dtype=jnp.int32)[None, :]).astype(jnp.bfloat16)


def block_order(n_grains, n_taps, grain):
    size = n_grains * n_taps * grain
    old = jnp.arange(size, dtype=jnp.int32)
    new = ((old // (n_taps * grain)) * grain + old % grain) * n_taps + (old // grain) % n_taps
    return (jnp.arange(size, dtype=jnp.int32)[:, None] == new[None, :]).astype(jnp.float32)


def on_device(volume, out_grad, kernel, sample_idx, a_inverse, g_inverse):
    highest = lax.Precision.HIGHEST
    f32 = jnp.float32
    channels = volume.shape[1]
    planes = volume.shape[2]
    y_cells = volume.shape[3]
    x_cells = volume.shape[4]
    cells = planes * y_cells * x_cells
    patch = kernel.shape[1]
    n_taps = patch // channels
    n_dp = lax.axis_size("dp")
    n_sp = lax.axis_size("space")
    row_ch = channels // n_dp
    col_ch = channels // n_sp
    grain = math.gcd(row_ch, col_ch)
    n_grains = channels // grain
    contract_cells = (((1,), (1,)), ((), ()))

    block = padded_2(volume, (("space", 2),), 1)
    padded = jnp.pad(block[0], ((0, 0), (0, 0), (1, 1), (1, 1)))
    slab = jnp.transpose(padded, (1, 2, 0, 3))
    patches_t = patch_matrix(slab, planes, y_cells, x_cells)
    grad_flat = out_grad[0].reshape(channels, cells)
    kernel_perm = kernel.reshape(channels, channels, n_taps).transpose(0, 2, 1).reshape(channels, patch)


    cell_ids = sample_idx[0]
    counts = jnp.sum(
        (cell_ids[:, None] == jnp.arange(cells, dtype=jnp.int32)[None, :]).astype(f32), axis=0
    )
    weighted = (patches_t.astype(f32) * counts[None, :]).astype(jnp.bfloat16)
    total_samples = sample_idx.shape[1] * n_sp * n_dp
    a_perm = lax.dot_general(
        weighted, patches_t, contract_cells, preferred_element_type=f32
    ) / jnp.float32(total_samples)
    rows = patch // n_dp
    cols = patch // n_sp
    order, placed, a_bf = lax.optimization_barrier(
        (tap_order(channels, n_taps), halving_order(channels, n_taps, rows, "dp"), a_perm.astype(jnp.bfloat16))
    )
    a_rows = jnp.dot(placed, a_bf, preferred_element_type=f32)
    a_orig, kernel_perm, grad_late = lax.optimization_barrier((a_rows, kernel_perm, grad_flat))
    grad_perm = lax.dot_general(grad_late, patches_t, contract_cells, preferred_element_type=f32)
    g_part = lax.dot_general(grad_late, grad_late, contract_cells, preferred_element_type=f32)
    terms = jnp.concatenate([grad_perm, g_part], axis=1)
    plane = butterfly_sum(terms, ("dp",))
    grad_plane = (
        plane[:, :patch].reshape(channels, n_taps, channels).transpose(0, 2, 1).reshape(channels, patch)
    )
    own_cols = quad_scatter(
        grad_plane.reshape(channels, n_sp, patch // n_sp), "space", 1, wire=f32
    ).reshape(channels, patch // n_sp)
    left = jnp.dot(g_inverse, own_cols, precision=highest)
    partial = jnp.dot(left, a_inverse, precision=highest)
    both = butterfly_sum(jnp.concatenate([partial, plane[:, patch:]], axis=1), ("space",))
    pre_grad = both[:, :patch]
    g_factor = both[:, patch:]
    forward = jnp.dot(kernel_perm, patches_t, preferred_element_type=f32)
    conv_out = forward.astype(jnp.bfloat16).reshape(1, channels, planes, y_cells, x_cells)
    step = 1
    while step < n_dp:
        half = a_orig.shape[0] // 2
        got = lax.ppermute(a_orig[half:].astype(jnp.bfloat16), "dp", partner("dp", step))
        a_orig = a_orig[:half] + got.astype(f32)
        step *= 2
    a_block = lax.dot_general(
        a_orig, order.astype(f32), contract_cells, precision=lax.Precision.HIGH
    )
    a_factor = quad_scatter(a_block.reshape(rows, n_sp, cols), "space", 1).reshape(rows, cols)
    return (conv_out, a_factor, g_factor, pre_grad)


def solution(mesh):
    placed = (
        P("dp", None, "space", None, None),
        P("dp", None, "space", None, None),
        P(),
        P("dp", "space"),
        P("space", None),
        P(),
    )
    return jax.shard_map(
        on_device,
        mesh=mesh,
        in_specs=placed,
        out_specs=(P("dp", None, "space", None, None), P("dp", "space"), P(), P()),
        check_vma=False,
    )
```

```python
import math

import jax
import jax.numpy as jnp
from jax import lax
from jax.experimental import pallas as pl
from jax.sharding import PartitionSpec as P


def padded_2(cells, sides, width):
    for axis, dim in sides:
        count = lax.axis_size(axis)
        ends = count - 1
        head = lax.slice_in_dim(cells, 0, width, axis=dim)
        tail = lax.slice_in_dim(cells, cells.shape[dim] - width, cells.shape[dim], axis=dim)
        cells = jnp.concatenate(
            [
                lax.ppermute(tail, axis, [(i, (i + 1) % count) for i in range(ends)]),
                cells,
                lax.ppermute(head, axis, [((i + 1) % count, i) for i in range(ends)]),
            ],
            axis=dim,
        )
    return cells


def partner(axis, step):
    return [(i, i ^ step) for i in range(lax.axis_size(axis))]


def butterfly_sum(x, axes):
    for axis in axes:
        size = lax.axis_size(axis)
        low = 1
        while low < size:
            high = low * 2
            got = lax.ppermute(x, axis, partner(axis, low))
            if high < size:
                pair = lax.ppermute(x, axis, partner(axis, high))
                other = lax.ppermute(x, axis, partner(axis, low + high))
                x = (x + got) + (pair + other)
                low = high * 2
            else:
                x = x + got
                low = high
    return x


def halving_scatter(blocks, axis, dim, wire=jnp.bfloat16):
    me = lax.axis_index(axis)
    step = 1
    while step < lax.axis_size(axis):
        shape = blocks.shape
        split = blocks.reshape(shape[:dim] + (shape[dim] // 2, 2) + shape[dim + 1 :])
        bit = (me // step) % 2
        keep = lax.dynamic_index_in_dim(split, bit, axis=dim + 1, keepdims=False)
        send = lax.dynamic_index_in_dim(split, 1 - bit, axis=dim + 1, keepdims=False)
        got = lax.ppermute(send.astype(wire), axis, partner(axis, step))
        blocks = keep + got.astype(jnp.float32)
        step *= 2
    return blocks


def quad_scatter(blocks, axis, dim, wire=jnp.bfloat16):
    me = lax.axis_index(axis)
    low = 1
    while low < lax.axis_size(axis):
        shape = blocks.shape
        if low * 2 < lax.axis_size(axis):
            split = blocks.reshape(shape[:dim] + (shape[dim] // 4, 4) + shape[dim + 1 :])
            digit = (me // low) % 4

            def pick(d):
                return lax.dynamic_index_in_dim(split, d, axis=dim + 1, keepdims=False)

            got = [
                lax.ppermute(pick(digit ^ k).astype(wire), axis, partner(axis, k * low)).astype(
                    jnp.float32
                )
                for k in (1, 2, 3)
            ]
            blocks = (pick(digit) + got[0]) + (got[1] + got[2])
            low *= 4
        else:
            split = blocks.reshape(shape[:dim] + (shape[dim] // 2, 2) + shape[dim + 1 :])
            bit = (me // low) % 2
            keep = lax.dynamic_index_in_dim(split, bit, axis=dim + 1, keepdims=False)
            send = lax.dynamic_index_in_dim(split, 1 - bit, axis=dim + 1, keepdims=False)
            got = lax.ppermute(send.astype(wire), axis, partner(axis, low))
            blocks = keep + got.astype(jnp.float32)
            low *= 2
    return blocks


def doubling_gather(x, axis):
    me = lax.axis_index(axis)
    step = 1
    while step < lax.axis_size(axis):
        other = lax.ppermute(x, axis, partner(axis, step))
        first = (me // step) % 2 == 0
        x = jnp.where(first, jnp.concatenate([x, other]), jnp.concatenate([other, x]))
        step *= 2
    return x


def patch_matrix(slab, planes, y_cells, x_cells):
    channels = slab.shape[2]
    cells = planes * y_cells * x_cells
    shifted = jnp.stack([slab[:, :, :, dx : dx + x_cells] for dx in range(3)])

    def body(src_ref, out_ref):
        dz = pl.program_id(0)
        for dy in range(3):
            for dx in range(3):
                row = (dy * 3 + dx) * channels
                for z in range(planes):
                    for y in range(y_cells):
                        out_ref[pl.ds(row, channels), pl.ds((z * y_cells + y) * x_cells, x_cells)] = (
                            src_ref[dx, z + dz, y + dy]
                        )

    return pl.pallas_call(
        body,
        grid=(3,),
        in_specs=[pl.BlockSpec(shifted.shape, lambda dz: (0, 0, 0, 0, 0))],
        out_specs=pl.BlockSpec((9 * channels, cells), lambda dz: (dz, 0)),
        out_shape=jax.ShapeDtypeStruct((27 * channels, cells), slab.dtype),
    )(shifted)


def tap_order(channels, n_taps):
    size = channels * n_taps
    new = jnp.arange(size, dtype=jnp.int32)
    old = (new % n_taps) * channels + new // n_taps
    return (old[:, None] == jnp.arange(size, dtype=jnp.int32)[None, :]).astype(jnp.bfloat16)


def halving_order(channels, n_taps, rows, axis):
    size = channels * n_taps
    bits = lax.axis_size(axis).bit_length() - 1
    spot = jnp.arange(size, dtype=jnp.int32)
    rank = spot // rows
    flipped = sum(((rank >> b) & 1) << (bits - 1 - b) for b in range(bits))
    block = jnp.bitwise_xor(flipped, lax.axis_index(axis))
    original = block * rows + spot % rows
    source = (original % n_taps) * channels + original // n_taps
    return (source[:, None] == jnp.arange(size, dtype=jnp.int32)[None, :]).astype(jnp.bfloat16)


def block_order(n_grains, n_taps, grain):
    size = n_grains * n_taps * grain
    old = jnp.arange(size, dtype=jnp.int32)
    new = ((old // (n_taps * grain)) * grain + old % grain) * n_taps + (old // grain) % n_taps
    return (jnp.arange(size, dtype=jnp.int32)[:, None] == new[None, :]).astype(jnp.float32)


def on_device(volume, out_grad, kernel, sample_idx, a_inverse, g_inverse):
    highest = lax.Precision.HIGHEST
    f32 = jnp.float32
    channels = volume.shape[1]
    planes = volume.shape[2]
    y_cells = volume.shape[3]
    x_cells = volume.shape[4]
    cells = planes * y_cells * x_cells
    patch = kernel.shape[1]
    n_taps = patch // channels
    n_dp = lax.axis_size("dp")
    n_sp = lax.axis_size("space")
    row_ch = channels // n_dp
    col_ch = channels // n_sp
    grain = math.gcd(row_ch, col_ch)
    n_grains = channels // grain
    contract_cells = (((1,), (1,)), ((), ()))

    block = padded_2(volume, (("space", 2),), 1)
    padded = jnp.pad(block[0], ((0, 0), (0, 0), (1, 1), (1, 1)))
    slab = jnp.transpose(padded, (1, 2, 0, 3))
    patches_t = patch_matrix(slab, planes, y_cells, x_cells)
    grad_flat = out_grad[0].reshape(channels, cells)
    kernel_perm = kernel.reshape(channels, channels, n_taps).transpose(0, 2, 1).reshape(channels, patch)

    grad_perm = lax.dot_general(grad_flat, patches_t, contract_cells, preferred_element_type=f32)
    g_part = lax.dot_general(grad_flat, grad_flat, contract_cells, preferred_element_type=f32)
    terms = jnp.concatenate([grad_perm, g_part], axis=1)
    terms, patches_t = lax.optimization_barrier((terms, patches_t))
    plane = butterfly_sum(terms, ("dp",))
    grad_plane = (
        plane[:, :patch].reshape(channels, n_taps, channels).transpose(0, 2, 1).reshape(channels, patch)
    )
    own_cols = quad_scatter(
        grad_plane.reshape(channels, n_sp, patch // n_sp), "space", 1, wire=f32
    ).reshape(channels, patch // n_sp)
    left = jnp.dot(g_inverse, own_cols, precision=highest)
    partial = jnp.dot(left, a_inverse, precision=highest)
    both = butterfly_sum(jnp.concatenate([partial, plane[:, patch:]], axis=1), ("space",))
    pre_grad = both[:, :patch]
    g_factor = both[:, patch:]


    cell_ids = sample_idx[0]
    counts = jnp.sum(
        (cell_ids[:, None] == jnp.arange(cells, dtype=jnp.int32)[None, :]).astype(f32), axis=0
    )
    weighted = (patches_t.astype(f32) * counts[None, :]).astype(jnp.bfloat16)
    total_samples = sample_idx.shape[1] * n_sp * n_dp
    split = patch // 2
    halves = [
        lax.dot_general(weighted, part, contract_cells, preferred_element_type=f32) / jnp.float32(total_samples)
        for part in (patches_t[:split], patches_t[split:])
    ]
    rows = patch // n_dp
    cols = patch // n_sp
    order, placed, left_bf = lax.optimization_barrier(
        (tap_order(channels, n_taps), halving_order(channels, n_taps, rows, "dp"), halves[0].astype(jnp.bfloat16))
    )
    left_rows = jnp.dot(placed, left_bf, preferred_element_type=f32)
    (right_bf,) = lax.optimization_barrier((halves[1].astype(jnp.bfloat16),))
    right_rows = jnp.dot(placed, right_bf, preferred_element_type=f32)
    left_rows, kernel_perm = lax.optimization_barrier((left_rows, kernel_perm))
    forward = jnp.dot(kernel_perm, patches_t, preferred_element_type=f32)
    conv_out = forward.astype(jnp.bfloat16).reshape(1, channels, planes, y_cells, x_cells)
    half = patch // 2
    summed = [
        part[:half] + lax.ppermute(part[half:].astype(jnp.bfloat16), "dp", partner("dp", 1)).astype(f32)
        for part in (left_rows, right_rows)
    ]
    a_orig = jnp.concatenate(summed, axis=1)
    step = 2
    while step < n_dp:
        half = a_orig.shape[0] // 2
        got = lax.ppermute(a_orig[half:].astype(jnp.bfloat16), "dp", partner("dp", step))
        a_orig = a_orig[:half] + got.astype(f32)
        step *= 2
    a_block = lax.dot_general(
        a_orig, order.astype(f32), contract_cells, precision=lax.Precision.HIGH
    )
    a_factor = quad_scatter(a_block.reshape(rows, n_sp, cols), "space", 1).reshape(rows, cols)
    return (conv_out, a_factor, g_factor, pre_grad)


def solution(mesh):
    placed = (
        P("dp", None, "space", None, None),
        P("dp", None, "space", None, None),
        P(),
        P("dp", "space"),
        P("space", None),
        P(),
    )
    return jax.shard_map(
        on_device,
        mesh=mesh,
        in_specs=placed,
        out_specs=(P("dp", None, "space", None, None), P("dp", "space"), P(), P()),
        check_vma=False,
    )
```

```python
import math

import jax
import jax.numpy as jnp
from jax import lax
from jax.experimental import pallas as pl
from jax.sharding import PartitionSpec as P


def padded_2(cells, sides, width):
    for axis, dim in sides:
        count = lax.axis_size(axis)
        ends = count - 1
        head = lax.slice_in_dim(cells, 0, width, axis=dim)
        tail = lax.slice_in_dim(cells, cells.shape[dim] - width, cells.shape[dim], axis=dim)
        cells = jnp.concatenate(
            [
                lax.ppermute(tail, axis, [(i, (i + 1) % count) for i in range(ends)]),
                cells,
                lax.ppermute(head, axis, [((i + 1) % count, i) for i in range(ends)]),
            ],
            axis=dim,
        )
    return cells


def partner(axis, step):
    return [(i, i ^ step) for i in range(lax.axis_size(axis))]


def butterfly_sum(x, axes):
    for axis in axes:
        size = lax.axis_size(axis)
        low = 1
        while low < size:
            high = low * 2
            got = lax.ppermute(x, axis, partner(axis, low))
            if high < size:
                pair = lax.ppermute(x, axis, partner(axis, high))
                other = lax.ppermute(x, axis, partner(axis, low + high))
                x = (x + got) + (pair + other)
                low = high * 2
            else:
                x = x + got
                low = high
    return x


def halving_scatter(blocks, axis, dim, wire=jnp.bfloat16):
    me = lax.axis_index(axis)
    step = 1
    while step < lax.axis_size(axis):
        shape = blocks.shape
        split = blocks.reshape(shape[:dim] + (shape[dim] // 2, 2) + shape[dim + 1 :])
        bit = (me // step) % 2
        keep = lax.dynamic_index_in_dim(split, bit, axis=dim + 1, keepdims=False)
        send = lax.dynamic_index_in_dim(split, 1 - bit, axis=dim + 1, keepdims=False)
        got = lax.ppermute(send.astype(wire), axis, partner(axis, step))
        blocks = keep + got.astype(jnp.float32)
        step *= 2
    return blocks


def quad_scatter(blocks, axis, dim, wire=jnp.bfloat16):
    me = lax.axis_index(axis)
    low = 1
    while low < lax.axis_size(axis):
        shape = blocks.shape
        if low * 2 < lax.axis_size(axis):
            split = blocks.reshape(shape[:dim] + (shape[dim] // 4, 4) + shape[dim + 1 :])
            digit = (me // low) % 4

            def pick(d):
                return lax.dynamic_index_in_dim(split, d, axis=dim + 1, keepdims=False)

            got = [
                lax.ppermute(pick(digit ^ k).astype(wire), axis, partner(axis, k * low)).astype(
                    jnp.float32
                )
                for k in (1, 2, 3)
            ]
            blocks = (pick(digit) + got[0]) + (got[1] + got[2])
            low *= 4
        else:
            split = blocks.reshape(shape[:dim] + (shape[dim] // 2, 2) + shape[dim + 1 :])
            bit = (me // low) % 2
            keep = lax.dynamic_index_in_dim(split, bit, axis=dim + 1, keepdims=False)
            send = lax.dynamic_index_in_dim(split, 1 - bit, axis=dim + 1, keepdims=False)
            got = lax.ppermute(send.astype(wire), axis, partner(axis, low))
            blocks = keep + got.astype(jnp.float32)
            low *= 2
    return blocks


def doubling_gather(x, axis):
    me = lax.axis_index(axis)
    step = 1
    while step < lax.axis_size(axis):
        other = lax.ppermute(x, axis, partner(axis, step))
        first = (me // step) % 2 == 0
        x = jnp.where(first, jnp.concatenate([x, other]), jnp.concatenate([other, x]))
        step *= 2
    return x


def patch_matrix(slab, planes, y_cells, x_cells):
    channels = slab.shape[2]
    cells = planes * y_cells * x_cells
    shifted = jnp.stack([slab[:, :, :, dx : dx + x_cells] for dx in range(3)])

    def body(src_ref, out_ref):
        for tap in range(27):
            dz, dy, dx = tap // 9, (tap // 3) % 3, tap % 3
            if True:
                row = tap * channels
                for z in range(planes):
                    for y in range(y_cells):
                        out_ref[pl.ds(row, channels), pl.ds((z * y_cells + y) * x_cells, x_cells)] = (
                            src_ref[dx, z + dz, y + dy]
                        )

    return pl.pallas_call(
        body,
        grid=(1,),
        in_specs=[pl.BlockSpec(shifted.shape, lambda i: (0, 0, 0, 0, 0))],
        out_specs=pl.BlockSpec((27 * channels, cells), lambda i: (0, 0)),
        out_shape=jax.ShapeDtypeStruct((27 * channels, cells), slab.dtype),
    )(shifted)


def tap_order(channels, n_taps):
    size = channels * n_taps
    new = jnp.arange(size, dtype=jnp.int32)
    old = (new % n_taps) * channels + new // n_taps
    return (old[:, None] == jnp.arange(size, dtype=jnp.int32)[None, :]).astype(jnp.bfloat16)


def halving_order(channels, n_taps, rows, axis):
    size = channels * n_taps
    bits = lax.axis_size(axis).bit_length() - 1
    spot = jnp.arange(size, dtype=jnp.int32)
    rank = spot // rows
    flipped = sum(((rank >> b) & 1) << (bits - 1 - b) for b in range(bits))
    block = jnp.bitwise_xor(flipped, lax.axis_index(axis))
    original = block * rows + spot % rows
    source = (original % n_taps) * channels + original // n_taps
    return (source[:, None] == jnp.arange(size, dtype=jnp.int32)[None, :]).astype(jnp.bfloat16)


def block_order(n_grains, n_taps, grain):
    size = n_grains * n_taps * grain
    old = jnp.arange(size, dtype=jnp.int32)
    new = ((old // (n_taps * grain)) * grain + old % grain) * n_taps + (old // grain) % n_taps
    return (jnp.arange(size, dtype=jnp.int32)[:, None] == new[None, :]).astype(jnp.float32)


def on_device(volume, out_grad, kernel, sample_idx, a_inverse, g_inverse):
    highest = lax.Precision.HIGHEST
    f32 = jnp.float32
    channels = volume.shape[1]
    planes = volume.shape[2]
    y_cells = volume.shape[3]
    x_cells = volume.shape[4]
    cells = planes * y_cells * x_cells
    patch = kernel.shape[1]
    n_taps = patch // channels
    n_dp = lax.axis_size("dp")
    n_sp = lax.axis_size("space")
    row_ch = channels // n_dp
    col_ch = channels // n_sp
    grain = math.gcd(row_ch, col_ch)
    n_grains = channels // grain
    contract_cells = (((1,), (1,)), ((), ()))

    block = padded_2(volume, (("space", 2),), 1)
    padded = jnp.pad(block[0], ((0, 0), (0, 0), (1, 1), (1, 1)))
    slab = jnp.transpose(padded, (1, 2, 0, 3))
    patches_t = patch_matrix(slab, planes, y_cells, x_cells)
    grad_flat = out_grad[0].reshape(channels, cells)
    kernel_perm = kernel.reshape(channels, channels, n_taps).transpose(0, 2, 1).reshape(channels, patch)

    grad_perm = lax.dot_general(grad_flat, patches_t, contract_cells, preferred_element_type=f32)
    g_part = lax.dot_general(grad_flat, grad_flat, contract_cells, preferred_element_type=f32)
    terms = jnp.concatenate([grad_perm, g_part], axis=1)
    terms, patches_t = lax.optimization_barrier((terms, patches_t))
    plane = butterfly_sum(terms, ("dp",))
    grad_plane = (
        plane[:, :patch].reshape(channels, n_taps, channels).transpose(0, 2, 1).reshape(channels, patch)
    )
    own_cols = quad_scatter(
        grad_plane.reshape(channels, n_sp, patch // n_sp), "space", 1, wire=f32
    ).reshape(channels, patch // n_sp)
    left = jnp.dot(g_inverse, own_cols, precision=highest)
    partial = jnp.dot(left, a_inverse, precision=highest)
    both = butterfly_sum(jnp.concatenate([partial, plane[:, patch:]], axis=1), ("space",))
    pre_grad = both[:, :patch]
    g_factor = both[:, patch:]


    cell_ids = sample_idx[0]
    counts = jnp.sum(
        (cell_ids[:, None] == jnp.arange(cells, dtype=jnp.int32)[None, :]).astype(f32), axis=0
    )
    weighted = (patches_t.astype(f32) * counts[None, :]).astype(jnp.bfloat16)
    total_samples = sample_idx.shape[1] * n_sp * n_dp
    a_perm = lax.dot_general(
        weighted, patches_t, contract_cells, preferred_element_type=f32
    ) / jnp.float32(total_samples)
    rows = patch // n_dp
    cols = patch // n_sp
    order, placed, a_bf = lax.optimization_barrier(
        (tap_order(channels, n_taps), halving_order(channels, n_taps, rows, "dp"), a_perm.astype(jnp.bfloat16))
    )
    a_rows = jnp.dot(placed, a_bf, preferred_element_type=f32)
    a_orig, kernel_perm = lax.optimization_barrier((a_rows, kernel_perm))
    forward = jnp.dot(kernel_perm, patches_t, preferred_element_type=f32)
    conv_out = forward.astype(jnp.bfloat16).reshape(1, channels, planes, y_cells, x_cells)
    step = 1
    while step < n_dp:
        half = a_orig.shape[0] // 2
        got = lax.ppermute(a_orig[half:].astype(jnp.bfloat16), "dp", partner("dp", step))
        a_orig = a_orig[:half] + got.astype(f32)
        step *= 2
    a_block = lax.dot_general(
        a_orig, order.astype(f32), contract_cells, precision=lax.Precision.HIGH
    )
    a_factor = quad_scatter(a_block.reshape(rows, n_sp, cols), "space", 1).reshape(rows, cols)
    return (conv_out, a_factor, g_factor, pre_grad)


def solution(mesh):
    placed = (
        P("dp", None, "space", None, None),
        P("dp", None, "space", None, None),
        P(),
        P("dp", "space"),
        P("space", None),
        P(),
    )
    return jax.shard_map(
        on_device,
        mesh=mesh,
        in_specs=placed,
        out_specs=(P("dp", None, "space", None, None), P("dp", "space"), P(), P()),
        check_vma=False,
    )
```
